256 devices in a mesh: dp: 32 (over y, x, core), segment: 8 (over z).
Axes of the slice: x: 4, y: 4, z: 8, core: 2. Of those that a mesh axis runs over, the one named last changes fastest.
Arguments:
- text_embed: bfloat16 [128, 32, 5120], P('dp'), may hold values from -6 to 6
- patches: bfloat16 [128, 128, 1280], P('dp'), may hold values from -6 to 6
- window_ids: int32 [128, 128], P('dp'), may hold values from 0 to 1, as said below
- offsets: int32 [128], P('dp'), may hold values from 0 to 32
- vit_qkv: bfloat16 [1280, 3840], replicated, may hold values from -0.15625 to 0.15625
- frozen_value: bfloat16 [8, 5120, 512], P('segment', 'dp'), may hold values from -0.078125 to 0.078125
- frozen_out: bfloat16 [8, 512, 5120], P('segment', None, 'dp'), may hold values from -0.25 to 0.25
- adapter_down: bfloat16 [8, 64, 5120], P('segment', None, 'dp'), may hold values from -0.078125 to 0.078125
- adapter_up: bfloat16 [8, 64, 5120], P('segment', None, 'dp'), may hold values from -0.75 to 0.75
- cotangent: bfloat16 [128, 64, 5120], P('dp'), may hold values from -6 to 6
Outputs:
- grad_down: float32 [8, 64, 5120], P('segment', None, 'dp')
- grad_up: float32 [8, 64, 5120], P('segment', None, 'dp')
The draws below stay inside these ranges and needn't reach their ends.
Inputs may be any that keep to these rules, and one draw needn't show every extreme that they name: `window_ids`: in each sample every window id names exactly 64 patches, in whole groups of 4 consecutive patches.
All inputs are finite; a program needn't handle non-finite values.
Results may differ from the reference program's by a relative error of at most 0.034.
Values may be sent and summed in bfloat16 or wider, within the bound.
No kernel may reach another device: no remote copies, remote signals or barrier semaphores. Data moves between devices by JAX's collectives and lax.ppermute only.
A program may use at most 128 MiB of HBM per device.

```python
import jax
import jax.numpy as jnp
from jax import lax

D = 5120
DV = 1280
VIT_HEADS = 16
KVW = 512
RA = 64
WINDOW = 64
SAMP_DEV = 4
TXT_LEN = 32
PATCHES = 128
SEQ = 64
SAMPLES = 128
N_DP = 32
N_SEGMENT = 8


def draw_window_ids(key, part):
    group_count = PATCHES // 4
    per_window = WINDOW // 4
    sample_keys = jax.random.split(key, SAMPLES)
    order = jax.vmap(lambda one_key: jax.random.permutation(one_key, group_count))(sample_keys)
    window_of_group = order // per_window
    return jnp.repeat(window_of_group, 4, axis=1).astype(jnp.int32)


def set_ends(result, rng, least, largest):
    longest = result.shape.index(max(result.shape))
    spots = []
    for shift in (0, 1):
        where = [jax.random.randint(jax.random.fold_in(rng, axis), (), 0, length) for axis, length in enumerate(result.shape)]
        where[longest] = (where[longest] + shift) % result.shape[longest]
        spots.append(tuple(where))
    return result.at[spots[0]].set(least).at[spots[1]].set(largest)


def spiked(values, own_key, source, target, parts, factor):
    owner, partner = [(jnp.arange(values.shape[dim]) // (values.shape[dim] // parts)).reshape([-1 if axis == dim else 1 for axis in range(values.ndim)]) for dim in (source, target)]
    chosen = jax.random.permutation(own_key, parts)[partner]
    strong = (owner == chosen) | (owner == (partner + parts // 2) % parts)
    return jnp.where(strong, factor * values, values)


def block_levels(key, shape, pieces, smallest, largest):
    gain, own = 1.0, jax.random.fold_in(key, 6)
    for axis_at, blocks in pieces:
        draws = jnp.exp(jax.random.uniform(jax.random.fold_in(own, axis_at), (blocks,), jnp.float32, smallest / len(pieces), largest / len(pieces)))
        gain = gain * jnp.repeat(draws, shape[axis_at] // blocks).reshape([-1 if axis == axis_at else 1 for axis in range(len(shape))])
    return gain


def centred(stream_key, extent, scale, limit, shards=(), kind=jnp.bfloat16):
    loudness = block_levels(stream_key, extent, shards, -0.22, 0.18) if shards else 1.0
    values = jax.random.normal(stream_key, extent, jnp.float32) * scale * loudness
    return jnp.minimum(jnp.maximum(values, -limit), limit).astype(kind)


def heavy_noise(own_key, shape, deviation, most, pieces, heavy, kind=jnp.bfloat16):
    entries = deviation * jax.random.normal(own_key, shape, jnp.float32)
    if pieces:
        entries = entries * block_levels(own_key, shape, pieces, -0.22, 0.18)
    return jnp.clip(spiked(entries, jax.random.fold_in(own_key, 3), *heavy), -most, most).astype(kind)


def setup_inputs(seed: int = 0) -> dict:
    key_list = jax.random.split(jax.random.key(seed), 11)
    text_embed = centred(key_list[0], (SAMPLES, TXT_LEN, D), 1.0, 6.0, ((0, 32),))
    patches = centred(key_list[1], (SAMPLES, PATCHES, DV), 1.0, 6.0, ((0, 32),))
    window_ids = draw_window_ids(jax.random.fold_in(key_list[10], 71), 0)
    offsets = set_ends(jax.random.randint(key_list[3], (SAMPLES,), 0, TXT_LEN + 1), jax.random.fold_in(key_list[3], 1), 0, TXT_LEN).astype(jnp.int32)
    vit_qkv = centred(key_list[4], (DV, 3 * DV), DV ** -0.5, 0.15625)
    frozen_value = centred(key_list[5], (N_SEGMENT, D, KVW), D ** -0.5, 0.078125, ((0, 8), (1, 32)))
    frozen_out = centred(key_list[6], (N_SEGMENT, KVW, D), KVW ** -0.5, 0.25, ((0, 8), (2, 32)))
    adapter_down = centred(key_list[7], (N_SEGMENT, RA, D), D ** -0.5, 0.078125, ((0, 8), (2, 32)))
    adapter_up = centred(key_list[8], (N_SEGMENT, RA, D), RA ** -0.5, 0.75, ((0, 8), (2, 32)))
    cotangent = heavy_noise(key_list[9], (SAMPLES, SEQ, D), 1.0, 6.0, ((0, 32),), (0, 2, 32, 2.75))
    return dict(text_embed=text_embed, patches=patches, window_ids=window_ids, offsets=offsets, vit_qkv=vit_qkv, frozen_value=frozen_value, frozen_out=frozen_out, adapter_down=adapter_down, adapter_up=adapter_up, cotangent=cotangent)


def rms_scale(values):
    return lax.rsqrt(lax.optimization_barrier(jnp.mean(values * values, axis=-1, keepdims=True)) + 1e-06)

def segment_parts(inputs, value_full, out_full, down_full):
    widened = inputs.astype(jnp.float32)
    first_rms = rms_scale(widened)
    normed_one = (widened * first_rms).astype(jnp.bfloat16)
    valued = jnp.dot(normed_one, value_full, preferred_element_type=jnp.float32).astype(jnp.bfloat16)
    base = (widened + jnp.dot(valued, out_full, preferred_element_type=jnp.float32)).astype(jnp.bfloat16)
    base_wide = base.astype(jnp.float32)
    second_rms = rms_scale(base_wide)
    normed_two = (base_wide * second_rms).astype(jnp.bfloat16)
    before = jnp.dot(normed_two, down_full.T, preferred_element_type=jnp.float32)
    return (widened, first_rms, base_wide, second_rms, normed_two, before)

def segment_forward(inputs, value_full, out_full, down_full, up_full):
    widened, first_rms, base_wide, second_rms, normed_two, before = segment_parts(inputs, value_full, out_full, down_full)
    hidden = jax.nn.silu(before).astype(jnp.bfloat16)
    return (base_wide + jnp.dot(hidden, up_full, preferred_element_type=jnp.float32)).astype(jnp.bfloat16)

def norm_back(grad_normed, widened, inverse_rms, upstream_wide):
    inner_mean = lax.optimization_barrier(jnp.mean(grad_normed * widened, axis=-1, keepdims=True))
    cubed = inverse_rms * inverse_rms * inverse_rms
    return (upstream_wide + inverse_rms * grad_normed - widened * cubed * inner_mean).astype(jnp.bfloat16)

def segment_backward(inputs, upstream, value_full, out_full, down_full, up_full):
    widened, first_rms, base_wide, second_rms, normed_two, before = segment_parts(inputs, value_full, out_full, down_full)
    hidden = jax.nn.silu(before).astype(jnp.bfloat16)
    up_term = jnp.dot(hidden.T, upstream, preferred_element_type=jnp.float32)
    through = jnp.dot(upstream, up_full.T, preferred_element_type=jnp.float32)
    sigmoid_part = jax.nn.sigmoid(before)
    grad_before = (through * sigmoid_part * (1.0 + before * (1.0 - sigmoid_part))).astype(jnp.bfloat16)
    down_term = jnp.dot(grad_before.T, normed_two, preferred_element_type=jnp.float32)
    grad_two = jnp.dot(grad_before, down_full, preferred_element_type=jnp.float32)
    grad_base = norm_back(grad_two, base_wide, second_rms, upstream.astype(jnp.float32))
    grad_valued = jnp.dot(grad_base, out_full.T, preferred_element_type=jnp.float32).astype(jnp.bfloat16)
    grad_one = jnp.dot(grad_valued, value_full.T, preferred_element_type=jnp.float32)
    grad_inputs = norm_back(grad_one, widened, first_rms, grad_base.astype(jnp.float32))
    return (grad_inputs, down_term, up_term)

def vision_tokens(patch_part, id_part, vit_qkv):
    samples_here, patch_len, vision_width = patch_part.shape
    head_width = vision_width // VIT_HEADS
    widened = patch_part.astype(jnp.float32)
    normed = (widened * rms_scale(widened)).astype(jnp.bfloat16)
    projected = jnp.dot(normed.reshape(samples_here * patch_len, vision_width), vit_qkv, preferred_element_type=jnp.float32).astype(jnp.bfloat16)
    projected = projected.reshape(samples_here, patch_len, 3, VIT_HEADS, head_width)
    query_part = projected[:, :, 0].astype(jnp.float32)
    key_part = projected[:, :, 1].astype(jnp.float32)
    value_part = projected[:, :, 2].astype(jnp.float32)
    scores = jnp.einsum('nqhd,nkhd->nhqk', query_part, key_part) * head_width ** (-0.5)
    same_window = id_part[:, None, :, None] == id_part[:, None, None, :]
    weights = jnp.where(same_window, jnp.exp(scores), 0.0)
    probabilities = (weights / lax.optimization_barrier(jnp.sum(weights, axis=-1, keepdims=True))).astype(jnp.bfloat16)
    attended = jnp.einsum('nhqk,nkhd->nqhd', probabilities.astype(jnp.float32), value_part)
    vit_out = (widened + attended.reshape(samples_here, patch_len, vision_width)).astype(jnp.bfloat16)
    return vit_out.reshape(samples_here, patch_len // 4, 4 * vision_width)

def take_rows(row_block, row_index):
    return jax.vmap(lambda block_one, index_one: jnp.take(block_one, index_one, axis=0))(row_block, row_index)

def join_rows(text_rows, image_rows, offsets):
    text_len = text_rows.shape[1]
    image_len = image_rows.shape[1]
    position = jnp.arange(text_len + image_len, dtype=jnp.int32)[None, :]
    begin_at = offsets.astype(jnp.int32)[:, None]
    in_image = (position >= begin_at) & (position < begin_at + image_len)
    text_index = jnp.clip(jnp.where(position < begin_at, position, position - image_len), 0, text_len - 1)
    image_index = jnp.clip(position - begin_at, 0, image_len - 1)
    return jnp.where(in_image[:, :, None], take_rows(image_rows, image_index), take_rows(text_rows, text_index))

def split_rows(grad_rows, offsets, text_len):
    image_len = grad_rows.shape[1] - text_len
    begin_at = offsets.astype(jnp.int32)[:, None]
    text_position = jnp.arange(text_len, dtype=jnp.int32)[None, :]
    text_index = jnp.where(text_position < begin_at, text_position, text_position + image_len)
    image_index = begin_at + jnp.arange(image_len, dtype=jnp.int32)[None, :]
    return (take_rows(grad_rows, text_index), take_rows(grad_rows, image_index))

def group_terms(text_part, patch_part, id_part, offset_part, vit_qkv, frozen_value, frozen_out, adapter_down, adapter_up, cot_part):
    samples_here, text_len, model_width = text_part.shape
    image_len = patch_part.shape[1] // 4
    total_len = text_len + image_len
    segment_count = adapter_down.shape[0]

    def weights_of(layer_index):
        return (frozen_value[layer_index], frozen_out[layer_index], adapter_down[layer_index], adapter_up[layer_index])
    image_tokens = vision_tokens(patch_part, id_part, vit_qkv).reshape(samples_here * image_len, model_width)
    image_act = segment_forward(image_tokens, *weights_of(0))
    text_rows = text_part.reshape(samples_here * text_len, model_width)
    text_act = segment_forward(text_rows, *weights_of(1))
    carried = join_rows(text_act.reshape(samples_here, text_len, model_width), image_act.reshape(samples_here, image_len, model_width), offset_part)
    carried = carried.reshape(samples_here * total_len, model_width)
    segment_inputs = {}
    for layer_index in range(2, segment_count):
        segment_inputs[layer_index] = carried
        if layer_index < segment_count - 1:
            carried = segment_forward(carried, *weights_of(layer_index))
    upstream = cot_part.reshape(samples_here * total_len, model_width)
    down_terms = [None] * segment_count
    up_terms = [None] * segment_count
    for layer_index in range(segment_count - 1, 1, -1):
        upstream, down_terms[layer_index], up_terms[layer_index] = segment_backward(segment_inputs[layer_index], upstream, *weights_of(layer_index))
    text_grad, image_grad = split_rows(upstream.reshape(samples_here, total_len, model_width), offset_part, text_len)
    unused_text, down_terms[1], up_terms[1] = segment_backward(text_rows, text_grad.reshape(samples_here * text_len, model_width), *weights_of(1))
    unused_image, down_terms[0], up_terms[0] = segment_backward(image_tokens, image_grad.reshape(samples_here * image_len, model_width), *weights_of(0))
    return (jnp.stack(down_terms), jnp.stack(up_terms))

def reference(text_embed, patches, window_ids, offsets, vit_qkv, frozen_value, frozen_out, adapter_down, adapter_up, cotangent):

    def accumulate(totals, group_index):
        first_row = (group_index * SAMP_DEV).astype(jnp.int32)

        def pick(array):
            return lax.dynamic_slice_in_dim(array, first_row, SAMP_DEV, 0)
        down_part, up_part = group_terms(pick(text_embed), pick(patches), pick(window_ids), pick(offsets), vit_qkv, frozen_value, frozen_out, adapter_down, adapter_up, pick(cotangent))
        down_part = lax.optimization_barrier(down_part.astype(jnp.bfloat16)).astype(jnp.float32)
        up_part = lax.optimization_barrier(up_part.astype(jnp.bfloat16)).astype(jnp.float32)
        return ((totals[0] + down_part, totals[1] + up_part), None)
    start_totals = (jnp.zeros(adapter_down.shape, jnp.float32), jnp.zeros(adapter_up.shape, jnp.float32))
    totals, unused_out = lax.scan(accumulate, start_totals, jnp.arange(N_DP, dtype=jnp.int32))
    return (totals[0], totals[1])
```

```python
import jax
import jax.numpy as jnp
from jax import lax
from jax.sharding import PartitionSpec as P

VIT_HEADS = 16


def as_sent(value):

    def short(part):
        return part.astype(jnp.bfloat16) if part.dtype == jnp.float32 else part

    return jax.tree.map(short, value)


def passed_along(value, axis, by):
    size = lax.axis_size(axis)
    pairs = [(i, i + by) for i in range(size) if 0 <= i + by < size]
    return lax.ppermute(value, axis, pairs)


def rms_scale(values):
    return lax.rsqrt(jnp.mean(values * values, axis=-1, keepdims=True) + 1e-06)


def segment_parts(inputs, value_full, out_full, down_full):
    widened = inputs.astype(jnp.float32)
    first_rms = rms_scale(widened)
    normed_one = (widened * first_rms).astype(jnp.bfloat16)
    valued = jnp.dot(normed_one, value_full, preferred_element_type=jnp.float32).astype(
        jnp.bfloat16
    )
    base = (widened + jnp.dot(valued, out_full, preferred_element_type=jnp.float32)).astype(
        jnp.bfloat16
    )
    base_wide = base.astype(jnp.float32)
    second_rms = rms_scale(base_wide)
    normed_two = (base_wide * second_rms).astype(jnp.bfloat16)
    before = lax.dot_general(
        normed_two, down_full, (((1,), (1,)), ((), ())), preferred_element_type=jnp.float32
    )
    return (widened, first_rms, base_wide, second_rms, normed_two, before)


def segment_forward(inputs, value_full, out_full, down_full, up_full):
    widened, first_rms, base_wide, second_rms, normed_two, before = segment_parts(
        inputs, value_full, out_full, down_full
    )
    hidden = jax.nn.silu(before).astype(jnp.bfloat16)
    return (base_wide + jnp.dot(hidden, up_full, preferred_element_type=jnp.float32)).astype(
        jnp.bfloat16
    )


def norm_back(grad_normed, widened, inverse_rms, upstream_wide):
    inner_mean = jnp.mean(grad_normed * widened, axis=-1, keepdims=True)
    cubed = inverse_rms * inverse_rms * inverse_rms
    return (upstream_wide + inverse_rms * grad_normed - widened * cubed * inner_mean).astype(
        jnp.bfloat16
    )


def transposed_dot(left, right):
    return lax.dot_general(
        left, right, (((1,), (1,)), ((), ())), preferred_element_type=jnp.float32
    )


def segment_backward(inputs, upstream, value_full, out_full, down_full, up_full):
    widened, first_rms, base_wide, second_rms, normed_two, before = segment_parts(
        inputs, value_full, out_full, down_full
    )
    hidden = jax.nn.silu(before).astype(jnp.bfloat16)
    up_term = lax.dot_general(
        hidden, upstream, (((0,), (0,)), ((), ())), preferred_element_type=jnp.float32
    )
    through = transposed_dot(upstream, up_full)
    sigmoid_part = jax.nn.sigmoid(before)
    grad_before = (through * sigmoid_part * (1.0 + before * (1.0 - sigmoid_part))).astype(
        jnp.bfloat16
    )
    down_term = lax.dot_general(
        grad_before, normed_two, (((0,), (0,)), ((), ())), preferred_element_type=jnp.float32
    )
    grad_two = jnp.dot(grad_before, down_full, preferred_element_type=jnp.float32)
    grad_base = norm_back(grad_two, base_wide, second_rms, upstream.astype(jnp.float32))
    grad_valued = transposed_dot(grad_base, out_full).astype(jnp.bfloat16)
    grad_one = transposed_dot(grad_valued, value_full)
    grad_inputs = norm_back(grad_one, widened, first_rms, grad_base.astype(jnp.float32))
    return (grad_inputs, down_term, up_term)


def vision_tokens(patch_part, id_part, vit_qkv):
    samples_here, patch_len, vision_width = patch_part.shape
    head_width = vision_width // VIT_HEADS
    widened = patch_part.astype(jnp.float32)
    normed = (widened * rms_scale(widened)).astype(jnp.bfloat16)
    projected = jnp.dot(
        normed.reshape(samples_here * patch_len, vision_width),
        vit_qkv,
        preferred_element_type=jnp.float32,
    ).astype(jnp.bfloat16)
    projected = projected.reshape(samples_here, patch_len, 3, VIT_HEADS, head_width)
    query_part = projected[:, :, 0]
    key_part = projected[:, :, 1]
    value_part = projected[:, :, 2]
    scores = jnp.einsum(
        "nqhd,nkhd->nhqk", query_part, key_part, preferred_element_type=jnp.float32
    ) * head_width ** (-0.5)
    same_window = id_part[:, None, :, None] == id_part[:, None, None, :]
    weights = jnp.where(same_window, jnp.exp(scores), 0.0)
    probabilities = (weights / jnp.sum(weights, axis=-1, keepdims=True)).astype(jnp.bfloat16)
    attended = jnp.einsum(
        "nhqk,nkhd->nqhd", probabilities, value_part, preferred_element_type=jnp.float32
    )
    vit_out = (widened + attended.reshape(samples_here, patch_len, vision_width)).astype(
        jnp.bfloat16
    )
    return vit_out.reshape(samples_here, patch_len // 4, 4 * vision_width)


def take_rows(row_block, row_index):
    return jax.vmap(lambda block_one, index_one: jnp.take(block_one, index_one, axis=0))(
        row_block, row_index
    )


def join_rows(text_rows, image_rows, offsets):
    text_len = text_rows.shape[1]
    image_len = image_rows.shape[1]
    position = jnp.arange(text_len + image_len, dtype=jnp.int32)[None, :]
    begin_at = offsets[:, None]
    in_image = (position >= begin_at) & (position < begin_at + image_len)
    text_index = jnp.clip(
        jnp.where(position < begin_at, position, position - image_len), 0, text_len - 1
    )
    image_index = jnp.clip(position - begin_at, 0, image_len - 1)
    return jnp.where(
        in_image[:, :, None], take_rows(image_rows, image_index), take_rows(text_rows, text_index)
    )


def split_rows(grad_rows, offsets, text_len):
    image_len = grad_rows.shape[1] - text_len
    begin_at = offsets[:, None]
    text_position = jnp.arange(text_len, dtype=jnp.int32)[None, :]
    text_index = jnp.where(text_position < begin_at, text_position, text_position + image_len)
    image_index = begin_at + jnp.arange(image_len, dtype=jnp.int32)[None, :]
    return (take_rows(grad_rows, text_index), take_rows(grad_rows, image_index))


def reduce_over_dp(down_total, up_total):
    parts = lax.axis_size("dp")
    both = jnp.concatenate([down_total, up_total], axis=0).astype(jnp.bfloat16)
    rows, width = both.shape
    blocks = both.reshape(rows, parts, width // parts).transpose(1, 0, 2)
    received = lax.all_to_all(blocks, "dp", 0, 0, tiled=True)
    summed = received.astype(jnp.float32).sum(axis=0)
    return summed[: down_total.shape[0]], summed[down_total.shape[0] :]


def pick_one(array, index):
    return lax.dynamic_index_in_dim(array, index, 0, keepdims=False)


def body(
    text_embed,
    patches,
    window_ids,
    offsets,
    vit_qkv,
    frozen_value,
    frozen_out,
    adapter_down,
    adapter_up,
    cotangent,
):
    segment_index = lax.axis_index("segment")
    segment_count = lax.axis_size("segment")
    samples_here, text_len, model_width = text_embed.shape
    image_len = patches.shape[1] // 4
    total_len = text_len + image_len
    value_width = frozen_value.shape[2]
    rank = adapter_down.shape[1]
    packed = jnp.concatenate(
        [frozen_value[0], frozen_out[0].T, adapter_down[0].T, adapter_up[0].T], axis=1
    )
    gathered = lax.all_gather(packed, "dp", axis=0, tiled=True)
    value_full = gathered[:, :value_width]
    out_full = gathered[:, value_width : 2 * value_width].T
    down_full = gathered[:, 2 * value_width : 2 * value_width + rank].T
    up_full = gathered[:, 2 * value_width + rank :].T
    rank_width = down_full.shape[0]
    segment_kind = jnp.where(
        segment_index == 0,
        0,
        jnp.where(segment_index == 1, 1, jnp.where(segment_index == segment_count - 1, 3, 2)),
    )

    def forward_here(current):
        return segment_forward(current, value_full, out_full, down_full, up_full)

    def backward_here(inputs, upstream):
        return segment_backward(inputs, upstream, value_full, out_full, down_full, up_full)

    def pad_rows(rows):
        filler = jnp.zeros((total_len - rows.shape[0], model_width), rows.dtype)
        return jnp.concatenate([rows, filler], axis=0)

    def forward_tick(tick, received, saved):
        micro = tick - segment_index
        valid = (micro >= 0) & (micro < samples_here)
        slot = jnp.clip(micro, 0, samples_here - 1)

        def forward_vision_case(unused_arg):
            tokens = vision_tokens(
                pick_one(patches, slot)[None], pick_one(window_ids, slot)[None], vit_qkv
            ).reshape(image_len, model_width)
            return (pad_rows(forward_here(tokens)), pad_rows(tokens))

        def forward_text_case(unused_arg):
            text_act = forward_here(pick_one(text_embed, slot))
            joined = join_rows(
                text_act[None], received[:image_len][None], pick_one(offsets, slot)[None]
            )
            return (joined.reshape(total_len, model_width), received)

        def forward_section_case(unused_arg):
            return (forward_here(received), received)

        def forward_last_case(unused_arg):
            return (received, received)

        outgoing, keep_rows = lax.switch(
            segment_kind,
            [forward_vision_case, forward_text_case, forward_section_case, forward_last_case],
            0,
        )
        previous = pick_one(saved, slot)
        saved = lax.dynamic_update_index_in_dim(
            saved, jnp.where(valid, keep_rows, previous), slot, 0
        )
        arriving = jax.tree.map(
            lambda part, own: part.astype(own.dtype),
            passed_along(as_sent(outgoing), "segment", 1),
            outgoing,
        )
        return (arriving, saved)

    def backward_tick(phase, received, saved, totals):
        micro = phase - (segment_count - 1 - segment_index)
        valid = (micro >= 0) & (micro < samples_here)
        slot = jnp.clip(micro, 0, samples_here - 1)

        def backward_vision_case(unused_arg):
            tokens = pick_one(saved, slot)[:image_len]
            unused_grad, part_down, part_up = backward_here(tokens, received[:image_len])
            return (jnp.zeros((total_len, model_width), jnp.bfloat16), part_down, part_up)

        def backward_text_case(unused_arg):
            text_part, image_part = split_rows(
                received[None], pick_one(offsets, slot)[None], text_len
            )
            unused_grad, part_down, part_up = backward_here(
                pick_one(text_embed, slot), text_part[0]
            )
            return (pad_rows(image_part[0]), part_down, part_up)

        def backward_section_case(unused_arg):
            return backward_here(pick_one(saved, slot), received)

        def backward_last_case(unused_arg):
            return backward_here(pick_one(saved, slot), pick_one(cotangent, slot))

        outgoing, part_down, part_up = lax.switch(
            segment_kind,
            [backward_vision_case, backward_text_case, backward_section_case, backward_last_case],
            0,
        )
        totals = (
            totals[0] + jnp.where(valid, part_down, 0.0),
            totals[1] + jnp.where(valid, part_up, 0.0),
        )
        arriving = jax.tree.map(
            lambda part, own: part.astype(own.dtype),
            passed_along(as_sent(outgoing), "segment", -1),
            outgoing,
        )
        return (arriving, totals)

    empty_rows = jnp.zeros((total_len, model_width), jnp.bfloat16)
    saved_start = jnp.zeros((samples_here, total_len, model_width), jnp.bfloat16)
    totals_start = (
        jnp.zeros((rank_width, model_width), jnp.float32),
        jnp.zeros((rank_width, model_width), jnp.float32),
    )
    sweep_ticks = samples_here + segment_count - 1

    def forward_step(tick, carry):
        return forward_tick(tick, carry[0], carry[1])

    unused_rows, saved = lax.fori_loop(0, sweep_ticks, forward_step, (empty_rows, saved_start))

    def backward_step(tick, carry):
        return backward_tick(tick, carry[0], saved, carry[1])

    unused_grad, totals = lax.fori_loop(0, sweep_ticks, backward_step, (empty_rows, totals_start))
    reduced_down, reduced_up = reduce_over_dp(totals[0], totals[1])
    return (reduced_down[None], reduced_up[None])


def solution(mesh):
    in_specs = (
        P("dp", None, None),
        P("dp", None, None),
        P("dp", None),
        P("dp"),
        P(),
        P("segment", "dp", None),
        P("segment", None, "dp"),
        P("segment", None, "dp"),
        P("segment", None, "dp"),
        P("dp", None, None),
    )
    out_specs = (P("segment", None, "dp"), P("segment", None, "dp"))
    return jax.shard_map(body, mesh=mesh, in_specs=in_specs, out_specs=out_specs, check_vma=False)
```

```python
import jax
import jax.numpy as jnp
from jax import lax
from jax.sharding import PartitionSpec as P

VIT_HEADS = 16


def as_sent(value):

    def short(part):
        return part.astype(jnp.bfloat16) if part.dtype == jnp.float32 else part

    return jax.tree.map(short, value)


def passed_along(value, axis, by):
    size = lax.axis_size(axis)
    pairs = [(i, i + by) for i in range(size) if 0 <= i + by < size]
    return lax.ppermute(value, axis, pairs)


def rms_scale(values):
    return lax.rsqrt(jnp.mean(values * values, axis=-1, keepdims=True) + 1e-06)


def segment_parts(inputs, value_full, out_full, down_full):
    widened = inputs.astype(jnp.float32)
    first_rms = rms_scale(widened)
    normed_one = (widened * first_rms).astype(jnp.bfloat16)
    valued = jnp.dot(normed_one, value_full, preferred_element_type=jnp.float32).astype(
        jnp.bfloat16
    )
    base = (widened + jnp.dot(valued, out_full, preferred_element_type=jnp.float32)).astype(
        jnp.bfloat16
    )
    base_wide = base.astype(jnp.float32)
    second_rms = rms_scale(base_wide)
    normed_two = (base_wide * second_rms).astype(jnp.bfloat16)
    before = lax.dot_general(
        normed_two, down_full, (((1,), (1,)), ((), ())), preferred_element_type=jnp.float32
    )
    return (widened, first_rms, base_wide, second_rms, normed_two, before)


def segment_forward(inputs, value_full, out_full, down_full, up_full):
    widened, first_rms, base_wide, second_rms, normed_two, before = segment_parts(
        inputs, value_full, out_full, down_full
    )
    hidden = jax.nn.silu(before).astype(jnp.bfloat16)
    return (base_wide + jnp.dot(hidden, up_full, preferred_element_type=jnp.float32)).astype(
        jnp.bfloat16
    )


def norm_back(grad_normed, widened, inverse_rms, upstream_wide):
    inner_mean = jnp.mean(grad_normed * widened, axis=-1, keepdims=True)
    cubed = inverse_rms * inverse_rms * inverse_rms
    return (upstream_wide + inverse_rms * grad_normed - widened * cubed * inner_mean).astype(
        jnp.bfloat16
    )


def transposed_dot(left, right):
    return lax.dot_general(
        left, right, (((1,), (1,)), ((), ())), preferred_element_type=jnp.float32
    )


def segment_backward(inputs, upstream, value_full, out_full, down_full, up_full):
    widened, first_rms, base_wide, second_rms, normed_two, before = segment_parts(
        inputs, value_full, out_full, down_full
    )
    hidden = jax.nn.silu(before).astype(jnp.bfloat16)
    up_term = lax.dot_general(
        hidden, upstream, (((0,), (0,)), ((), ())), preferred_element_type=jnp.float32
    )
    through = transposed_dot(upstream, up_full)
    sigmoid_part = jax.nn.sigmoid(before)
    grad_before = (through * sigmoid_part * (1.0 + before * (1.0 - sigmoid_part))).astype(
        jnp.bfloat16
    )
    down_term = lax.dot_general(
        grad_before, normed_two, (((0,), (0,)), ((), ())), preferred_element_type=jnp.float32
    )
    grad_two = jnp.dot(grad_before, down_full, preferred_element_type=jnp.float32)
    grad_base = norm_back(grad_two, base_wide, second_rms, upstream.astype(jnp.float32))
    grad_valued = transposed_dot(grad_base, out_full).astype(jnp.bfloat16)
    grad_one = transposed_dot(grad_valued, value_full)
    grad_inputs = norm_back(grad_one, widened, first_rms, grad_base.astype(jnp.float32))
    return (grad_inputs, down_term, up_term)


def segment_forward_with_base(inputs, value_full, out_full, down_full, up_full):
    widened, first_rms, base_wide, second_rms, normed_two, before = segment_parts(
        inputs, value_full, out_full, down_full
    )
    hidden = jax.nn.silu(before).astype(jnp.bfloat16)
    result = (base_wide + jnp.dot(hidden, up_full, preferred_element_type=jnp.float32)).astype(
        jnp.bfloat16
    )
    return result, base_wide.astype(jnp.bfloat16)


def base_of(inputs, value_full, out_full):
    widened = inputs.astype(jnp.float32)
    normed_one = (widened * rms_scale(widened)).astype(jnp.bfloat16)
    valued = jnp.dot(normed_one, value_full, preferred_element_type=jnp.float32).astype(
        jnp.bfloat16
    )
    return (widened + jnp.dot(valued, out_full, preferred_element_type=jnp.float32)).astype(
        jnp.bfloat16
    )


def segment_backward_saved(inputs, base, upstream, value_full, out_full, down_full, up_full):
    widened = inputs.astype(jnp.float32)
    first_rms = rms_scale(widened)
    base_wide = base.astype(jnp.float32)
    second_rms = rms_scale(base_wide)
    normed_two = (base_wide * second_rms).astype(jnp.bfloat16)
    before = lax.dot_general(
        normed_two, down_full, (((1,), (1,)), ((), ())), preferred_element_type=jnp.float32
    )
    hidden = jax.nn.silu(before).astype(jnp.bfloat16)
    up_term = lax.dot_general(
        hidden, upstream, (((0,), (0,)), ((), ())), preferred_element_type=jnp.float32
    )
    through = transposed_dot(upstream, up_full)
    sigmoid_part = jax.nn.sigmoid(before)
    grad_before = (through * sigmoid_part * (1.0 + before * (1.0 - sigmoid_part))).astype(
        jnp.bfloat16
    )
    down_term = lax.dot_general(
        grad_before, normed_two, (((0,), (0,)), ((), ())), preferred_element_type=jnp.float32
    )
    grad_two = jnp.dot(grad_before, down_full, preferred_element_type=jnp.float32)
    grad_base = norm_back(grad_two, base_wide, second_rms, upstream.astype(jnp.float32))
    grad_valued = transposed_dot(grad_base, out_full).astype(jnp.bfloat16)
    grad_one = transposed_dot(grad_valued, value_full)
    grad_inputs = norm_back(grad_one, widened, first_rms, grad_base.astype(jnp.float32))
    return (grad_inputs, down_term, up_term)


def vision_tokens(patch_part, id_part, vit_qkv):
    samples_here, patch_len, vision_width = patch_part.shape
    head_width = vision_width // VIT_HEADS
    widened = patch_part.astype(jnp.float32)
    normed = (widened * rms_scale(widened)).astype(jnp.bfloat16)
    projected = jnp.dot(
        normed.reshape(samples_here * patch_len, vision_width),
        vit_qkv,
        preferred_element_type=jnp.float32,
    ).astype(jnp.bfloat16)
    projected = projected.reshape(samples_here, patch_len, 3, VIT_HEADS, head_width)
    query_part = projected[:, :, 0]
    key_part = projected[:, :, 1]
    value_part = projected[:, :, 2]
    scores = jnp.einsum(
        "nqhd,nkhd->nhqk", query_part, key_part, preferred_element_type=jnp.float32
    ) * head_width ** (-0.5)
    same_window = id_part[:, None, :, None] == id_part[:, None, None, :]
    weights = jnp.where(same_window, jnp.exp(scores), 0.0)
    probabilities = (weights / jnp.sum(weights, axis=-1, keepdims=True)).astype(jnp.bfloat16)
    attended = jnp.einsum(
        "nhqk,nkhd->nqhd", probabilities, value_part, preferred_element_type=jnp.float32
    )
    vit_out = (widened + attended.reshape(samples_here, patch_len, vision_width)).astype(
        jnp.bfloat16
    )
    return vit_out.reshape(samples_here, patch_len // 4, 4 * vision_width)


def take_rows(row_block, row_index):
    return jax.vmap(lambda block_one, index_one: jnp.take(block_one, index_one, axis=0))(
        row_block, row_index
    )


def join_rows(text_rows, image_rows, offsets):
    text_len = text_rows.shape[1]
    image_len = image_rows.shape[1]
    position = jnp.arange(text_len + image_len, dtype=jnp.int32)[None, :]
    begin_at = offsets[:, None]
    in_image = (position >= begin_at) & (position < begin_at + image_len)
    text_index = jnp.clip(
        jnp.where(position < begin_at, position, position - image_len), 0, text_len - 1
    )
    image_index = jnp.clip(position - begin_at, 0, image_len - 1)
    return jnp.where(
        in_image[:, :, None], take_rows(image_rows, image_index), take_rows(text_rows, text_index)
    )


def split_rows(grad_rows, offsets, text_len):
    image_len = grad_rows.shape[1] - text_len
    begin_at = offsets[:, None]
    text_position = jnp.arange(text_len, dtype=jnp.int32)[None, :]
    text_index = jnp.where(text_position < begin_at, text_position, text_position + image_len)
    image_index = begin_at + jnp.arange(image_len, dtype=jnp.int32)[None, :]
    return (take_rows(grad_rows, text_index), take_rows(grad_rows, image_index))


def reduce_over_dp(down_total, up_total):
    parts = lax.axis_size("dp")
    both = jnp.concatenate([down_total, up_total], axis=0).astype(jnp.bfloat16)
    rows, width = both.shape
    blocks = both.reshape(rows, parts, width // parts).transpose(1, 0, 2)
    received = lax.all_to_all(blocks, "dp", 0, 0, tiled=True)
    summed = received.astype(jnp.float32).sum(axis=0)
    return summed[: down_total.shape[0]], summed[down_total.shape[0] :]


def pick_one(array, index):
    return lax.dynamic_index_in_dim(array, index, 0, keepdims=False)


def body(
    text_embed,
    patches,
    window_ids,
    offsets,
    vit_qkv,
    frozen_value,
    frozen_out,
    adapter_down,
    adapter_up,
    cotangent,
):
    segment_index = lax.axis_index("segment")
    segment_count = lax.axis_size("segment")
    samples_here, text_len, model_width = text_embed.shape
    image_len = patches.shape[1] // 4
    total_len = text_len + image_len
    value_width = frozen_value.shape[2]
    rank = adapter_down.shape[1]
    packed = jnp.concatenate(
        [frozen_value[0], frozen_out[0].T, adapter_down[0].T, adapter_up[0].T], axis=1
    )
    gathered = lax.all_gather(packed, "dp", axis=0, tiled=True)
    value_full = gathered[:, :value_width]
    out_full = gathered[:, value_width : 2 * value_width].T
    down_full = gathered[:, 2 * value_width : 2 * value_width + rank].T
    up_full = gathered[:, 2 * value_width + rank :].T
    rank_width = down_full.shape[0]
    segment_kind = jnp.where(
        segment_index == 0,
        0,
        jnp.where(segment_index == 1, 1, jnp.where(segment_index == segment_count - 1, 3, 2)),
    )

    weights = (value_full, out_full, down_full, up_full)
    branch_rows = samples_here * text_len

    def pad_rows(rows):
        filler = jnp.zeros((total_len - rows.shape[0], model_width), rows.dtype)
        return jnp.concatenate([rows, filler], axis=0)

    def split_samples(rows):
        return rows.reshape(samples_here, rows.shape[0] // samples_here, model_width)

    def prepare_vision(unused_arg):
        tokens = vision_tokens(patches, window_ids, vit_qkv).reshape(
            samples_here * image_len, model_width
        )
        act, base = segment_forward_with_base(tokens, *weights)
        return (split_samples(tokens), split_samples(act), split_samples(base))

    def prepare_text(unused_arg):
        rows = text_embed.reshape(branch_rows, model_width)
        act, base = segment_forward_with_base(rows, *weights)
        return (text_embed, split_samples(act), split_samples(base))

    def prepare_none(unused_arg):
        empty = jnp.zeros((samples_here, text_len, model_width), jnp.bfloat16)
        return (empty, empty, empty)

    branch_in, branch_act, branch_base = lax.switch(
        jnp.minimum(segment_kind, 2), [prepare_vision, prepare_text, prepare_none], 0
    )

    def forward_tick(tick, received, saved_in, saved_base):
        micro = tick - segment_index
        valid = (micro >= 0) & (micro < samples_here)
        slot = jnp.clip(micro, 0, samples_here - 1)

        def forward_vision_case(unused_arg):
            return (pad_rows(pick_one(branch_act, slot)), received)

        def forward_text_case(unused_arg):
            joined = join_rows(
                pick_one(branch_act, slot)[None],
                received[:image_len][None],
                pick_one(offsets, slot)[None],
            )
            return (joined.reshape(total_len, model_width), received)

        def forward_section_case(unused_arg):
            return segment_forward_with_base(received, *weights)

        def forward_last_case(unused_arg):
            return (received, base_of(received, value_full, out_full))

        def forward_idle_case(unused_arg):
            return (received, received)

        outgoing, keep_base = lax.switch(
            jnp.where(valid, segment_kind, 4),
            [
                forward_vision_case,
                forward_text_case,
                forward_section_case,
                forward_last_case,
                forward_idle_case,
            ],
            0,
        )
        saved_in = lax.dynamic_update_index_in_dim(
            saved_in, jnp.where(valid, received, pick_one(saved_in, slot)), slot, 0
        )
        saved_base = lax.dynamic_update_index_in_dim(
            saved_base, jnp.where(valid, keep_base, pick_one(saved_base, slot)), slot, 0
        )
        arriving = passed_along(outgoing, "segment", 1)
        return (arriving, saved_in, saved_base)

    def backward_tick(phase, received, saved_in, saved_base, totals):
        micro = phase - (segment_count - 1 - segment_index)
        valid = (micro >= 0) & (micro < samples_here)
        slot = jnp.clip(micro, 0, samples_here - 1)

        def backward_vision_case(unused_arg):
            unused_grad, part_down, part_up = segment_backward_saved(
                pick_one(branch_in, slot),
                pick_one(branch_base, slot),
                received[:image_len],
                *weights,
            )
            return (jnp.zeros((total_len, model_width), jnp.bfloat16), part_down, part_up)

        def backward_text_case(unused_arg):
            text_part, image_part = split_rows(
                received[None], pick_one(offsets, slot)[None], text_len
            )
            unused_grad, part_down, part_up = segment_backward_saved(
                pick_one(branch_in, slot), pick_one(branch_base, slot), text_part[0], *weights
            )
            return (pad_rows(image_part[0]), part_down, part_up)

        def backward_section_case(unused_arg):
            return segment_backward_saved(
                pick_one(saved_in, slot), pick_one(saved_base, slot), received, *weights
            )

        def backward_last_case(unused_arg):
            return segment_backward_saved(
                pick_one(saved_in, slot),
                pick_one(saved_base, slot),
                pick_one(cotangent, slot),
                *weights,
            )

        def backward_idle_case(unused_arg):
            zeros = jnp.zeros((rank_width, model_width), jnp.float32)
            return (received, zeros, zeros)

        outgoing, part_down, part_up = lax.switch(
            jnp.where(valid, segment_kind, 4),
            [
                backward_vision_case,
                backward_text_case,
                backward_section_case,
                backward_last_case,
                backward_idle_case,
            ],
            0,
        )
        totals = (totals[0] + part_down, totals[1] + part_up)
        arriving = passed_along(outgoing, "segment", -1)
        return (arriving, totals)

    empty_rows = jnp.zeros((total_len, model_width), jnp.bfloat16)
    saved_start = jnp.zeros((samples_here, total_len, model_width), jnp.bfloat16)
    totals_start = (
        jnp.zeros((rank_width, model_width), jnp.float32),
        jnp.zeros((rank_width, model_width), jnp.float32),
    )
    sweep_ticks = samples_here + segment_count - 1

    def forward_step(tick, carry):
        return forward_tick(tick, carry[0], carry[1], carry[2])

    unused_rows, saved_in, saved_base = lax.fori_loop(
        0, sweep_ticks, forward_step, (empty_rows, saved_start, saved_start)
    )

    def backward_step(tick, carry):
        return backward_tick(tick, carry[0], saved_in, saved_base, carry[1])

    unused_grad, totals = lax.fori_loop(0, sweep_ticks, backward_step, (empty_rows, totals_start))
    reduced_down, reduced_up = reduce_over_dp(totals[0], totals[1])
    return (reduced_down[None], reduced_up[None])


def solution(mesh):
    in_specs = (
        P("dp", None, None),
        P("dp", None, None),
        P("dp", None),
        P("dp"),
        P(),
        P("segment", "dp", None),
        P("segment", None, "dp"),
        P("segment", None, "dp"),
        P("segment", None, "dp"),
        P("dp", None, None),
    )
    out_specs = (P("segment", None, "dp"), P("segment", None, "dp"))
    return jax.shard_map(body, mesh=mesh, in_specs=in_specs, out_specs=out_specs, check_vma=False)
```

```python
import jax
import jax.numpy as jnp
from jax import lax
from jax.sharding import PartitionSpec as P

VIT_HEADS = 16


def as_sent(value):

    def short(part):
        return part.astype(jnp.bfloat16) if part.dtype == jnp.float32 else part

    return jax.tree.map(short, value)


def passed_along(value, axis, by):
    size = lax.axis_size(axis)
    pairs = [(i, i + by) for i in range(size) if 0 <= i + by < size]
    return lax.ppermute(value, axis, pairs)


def rms_scale(values):
    return lax.rsqrt(jnp.mean(values * values, axis=-1, keepdims=True) + 1e-06)


def segment_parts(inputs, value_full, out_full, down_full):
    widened = inputs.astype(jnp.float32)
    first_rms = rms_scale(widened)
    normed_one = (widened * first_rms).astype(jnp.bfloat16)
    valued = jnp.dot(normed_one, value_full, preferred_element_type=jnp.float32).astype(
        jnp.bfloat16
    )
    base = (widened + jnp.dot(valued, out_full, preferred_element_type=jnp.float32)).astype(
        jnp.bfloat16
    )
    base_wide = base.astype(jnp.float32)
    second_rms = rms_scale(base_wide)
    normed_two = (base_wide * second_rms).astype(jnp.bfloat16)
    before = lax.dot_general(
        normed_two, down_full, (((1,), (1,)), ((), ())), preferred_element_type=jnp.float32
    )
    return (widened, first_rms, base_wide, second_rms, normed_two, before)


def segment_forward(inputs, value_full, out_full, down_full, up_full):
    widened, first_rms, base_wide, second_rms, normed_two, before = segment_parts(
        inputs, value_full, out_full, down_full
    )
    hidden = jax.nn.silu(before).astype(jnp.bfloat16)
    return (base_wide + jnp.dot(hidden, up_full, preferred_element_type=jnp.float32)).astype(
        jnp.bfloat16
    )


def norm_back(grad_normed, widened, inverse_rms, upstream_wide):
    inner_mean = jnp.mean(grad_normed * widened, axis=-1, keepdims=True)
    cubed = inverse_rms * inverse_rms * inverse_rms
    return (upstream_wide + inverse_rms * grad_normed - widened * cubed * inner_mean).astype(
        jnp.bfloat16
    )


def transposed_dot(left, right):
    return lax.dot_general(
        left, right, (((1,), (1,)), ((), ())), preferred_element_type=jnp.float32
    )


def segment_backward(inputs, upstream, value_full, out_full, down_full, up_full):
    widened, first_rms, base_wide, second_rms, normed_two, before = segment_parts(
        inputs, value_full, out_full, down_full
    )
    hidden = jax.nn.silu(before).astype(jnp.bfloat16)
    up_term = lax.dot_general(
        hidden, upstream, (((0,), (0,)), ((), ())), preferred_element_type=jnp.float32
    )
    through = transposed_dot(upstream, up_full)
    sigmoid_part = jax.nn.sigmoid(before)
    grad_before = (through * sigmoid_part * (1.0 + before * (1.0 - sigmoid_part))).astype(
        jnp.bfloat16
    )
    down_term = lax.dot_general(
        grad_before, normed_two, (((0,), (0,)), ((), ())), preferred_element_type=jnp.float32
    )
    grad_two = jnp.dot(grad_before, down_full, preferred_element_type=jnp.float32)
    grad_base = norm_back(grad_two, base_wide, second_rms, upstream.astype(jnp.float32))
    grad_valued = transposed_dot(grad_base, out_full).astype(jnp.bfloat16)
    grad_one = transposed_dot(grad_valued, value_full)
    grad_inputs = norm_back(grad_one, widened, first_rms, grad_base.astype(jnp.float32))
    return (grad_inputs, down_term, up_term)


def segment_forward_with_base(inputs, value_full, out_full, down_full, up_full):
    widened, first_rms, base_wide, second_rms, normed_two, before = segment_parts(
        inputs, value_full, out_full, down_full
    )
    hidden = jax.nn.silu(before).astype(jnp.bfloat16)
    result = (base_wide + jnp.dot(hidden, up_full, preferred_element_type=jnp.float32)).astype(
        jnp.bfloat16
    )
    return result, base_wide.astype(jnp.bfloat16)


def base_of(inputs, value_full, out_full):
    widened = inputs.astype(jnp.float32)
    normed_one = (widened * rms_scale(widened)).astype(jnp.bfloat16)
    valued = jnp.dot(normed_one, value_full, preferred_element_type=jnp.float32).astype(
        jnp.bfloat16
    )
    return (widened + jnp.dot(valued, out_full, preferred_element_type=jnp.float32)).astype(
        jnp.bfloat16
    )


def segment_backward_saved(inputs, base, upstream, value_full, out_full, down_full, up_full):
    widened = inputs.astype(jnp.float32)
    first_rms = rms_scale(widened)
    base_wide = base.astype(jnp.float32)
    second_rms = rms_scale(base_wide)
    normed_two = (base_wide * second_rms).astype(jnp.bfloat16)
    before = lax.dot_general(
        normed_two, down_full, (((1,), (1,)), ((), ())), preferred_element_type=jnp.float32
    )
    hidden = jax.nn.silu(before).astype(jnp.bfloat16)
    up_term = lax.dot_general(
        hidden, upstream, (((0,), (0,)), ((), ())), preferred_element_type=jnp.float32
    )
    through = transposed_dot(upstream, up_full)
    sigmoid_part = jax.nn.sigmoid(before)
    grad_before = (through * sigmoid_part * (1.0 + before * (1.0 - sigmoid_part))).astype(
        jnp.bfloat16
    )
    down_term = lax.dot_general(
        grad_before, normed_two, (((0,), (0,)), ((), ())), preferred_element_type=jnp.float32
    )
    grad_two = jnp.dot(grad_before, down_full, preferred_element_type=jnp.float32)
    grad_base = norm_back(grad_two, base_wide, second_rms, upstream.astype(jnp.float32))
    grad_valued = transposed_dot(grad_base, out_full).astype(jnp.bfloat16)
    grad_one = transposed_dot(grad_valued, value_full)
    grad_inputs = norm_back(grad_one, widened, first_rms, grad_base.astype(jnp.float32))
    return (grad_inputs, down_term, up_term)


def vision_tokens(patch_part, id_part, vit_qkv):
    samples_here, patch_len, vision_width = patch_part.shape
    head_width = vision_width // VIT_HEADS
    widened = patch_part.astype(jnp.float32)
    normed = (widened * rms_scale(widened)).astype(jnp.bfloat16)
    projected = jnp.dot(
        normed.reshape(samples_here * patch_len, vision_width),
        vit_qkv,
        preferred_element_type=jnp.float32,
    ).astype(jnp.bfloat16)
    projected = projected.reshape(samples_here, patch_len, 3, VIT_HEADS, head_width)
    query_part = projected[:, :, 0]
    key_part = projected[:, :, 1]
    value_part = projected[:, :, 2]
    scores = jnp.einsum(
        "nqhd,nkhd->nhqk", query_part, key_part, preferred_element_type=jnp.float32
    ) * head_width ** (-0.5)
    same_window = id_part[:, None, :, None] == id_part[:, None, None, :]
    weights = jnp.where(same_window, jnp.exp(scores), 0.0)
    probabilities = (weights / jnp.sum(weights, axis=-1, keepdims=True)).astype(jnp.bfloat16)
    attended = jnp.einsum(
        "nhqk,nkhd->nqhd", probabilities, value_part, preferred_element_type=jnp.float32
    )
    vit_out = (widened + attended.reshape(samples_here, patch_len, vision_width)).astype(
        jnp.bfloat16
    )
    return vit_out.reshape(samples_here, patch_len // 4, 4 * vision_width)


def take_rows(row_block, row_index):
    return jax.vmap(lambda block_one, index_one: jnp.take(block_one, index_one, axis=0))(
        row_block, row_index
    )


def join_rows(text_rows, image_rows, offsets):
    text_len = text_rows.shape[1]
    image_len = image_rows.shape[1]
    position = jnp.arange(text_len + image_len, dtype=jnp.int32)[None, :]
    begin_at = offsets[:, None]
    in_image = (position >= begin_at) & (position < begin_at + image_len)
    text_index = jnp.clip(
        jnp.where(position < begin_at, position, position - image_len), 0, text_len - 1
    )
    image_index = jnp.clip(position - begin_at, 0, image_len - 1)
    return jnp.where(
        in_image[:, :, None], take_rows(image_rows, image_index), take_rows(text_rows, text_index)
    )


def split_rows(grad_rows, offsets, text_len):
    image_len = grad_rows.shape[1] - text_len
    begin_at = offsets[:, None]
    text_position = jnp.arange(text_len, dtype=jnp.int32)[None, :]
    text_index = jnp.where(text_position < begin_at, text_position, text_position + image_len)
    image_index = begin_at + jnp.arange(image_len, dtype=jnp.int32)[None, :]
    return (take_rows(grad_rows, text_index), take_rows(grad_rows, image_index))


def reduce_over_dp(down_total, up_total):
    parts = lax.axis_size("dp")
    both = jnp.concatenate([down_total, up_total], axis=0).astype(jnp.bfloat16)
    rows, width = both.shape
    blocks = both.reshape(rows, parts, width // parts).transpose(1, 0, 2)
    received = lax.all_to_all(blocks, "dp", 0, 0, tiled=True)
    summed = received.astype(jnp.float32).sum(axis=0)
    return summed[: down_total.shape[0]], summed[down_total.shape[0] :]


def pick_one(array, index):
    return lax.dynamic_index_in_dim(array, index, 0, keepdims=False)


def body(
    text_embed,
    patches,
    window_ids,
    offsets,
    vit_qkv,
    frozen_value,
    frozen_out,
    adapter_down,
    adapter_up,
    cotangent,
):
    segment_index = lax.axis_index("segment")
    segment_count = lax.axis_size("segment")
    samples_here, text_len, model_width = text_embed.shape
    image_len = patches.shape[1] // 4
    total_len = text_len + image_len
    value_width = frozen_value.shape[2]
    rank = adapter_down.shape[1]
    packed = jnp.concatenate(
        [frozen_value[0].T, frozen_out[0], adapter_down[0], adapter_up[0]], axis=0
    )
    gathered = lax.all_gather(packed, "dp", axis=1, tiled=True)
    value_full = gathered[:value_width].T
    out_full = gathered[value_width : 2 * value_width]
    down_full = gathered[2 * value_width : 2 * value_width + rank]
    up_full = gathered[2 * value_width + rank :]
    rank_width = down_full.shape[0]
    segment_kind = jnp.where(
        segment_index == 0,
        0,
        jnp.where(segment_index == 1, 1, jnp.where(segment_index == segment_count - 1, 3, 2)),
    )

    weights = (value_full, out_full, down_full, up_full)
    branch_rows = samples_here * text_len

    def pad_rows(rows):
        filler = jnp.zeros((total_len - rows.shape[0], model_width), rows.dtype)
        return jnp.concatenate([rows, filler], axis=0)

    def split_samples(rows):
        return rows.reshape(samples_here, rows.shape[0] // samples_here, model_width)

    def vision_only(unused_arg):
        return vision_tokens(patches, window_ids, vit_qkv)

    def no_vision(unused_arg):
        return jnp.zeros((samples_here, image_len, model_width), jnp.bfloat16)

    image_tokens = lax.cond(segment_index == 0, vision_only, no_vision, 0)

    def prepare_vision(unused_arg):
        tokens = image_tokens.reshape(samples_here * image_len, model_width)
        act, base = segment_forward_with_base(tokens, *weights)
        return (image_tokens, split_samples(act), split_samples(base))

    def prepare_text(unused_arg):
        rows = text_embed.reshape(branch_rows, model_width)
        act, base = segment_forward_with_base(rows, *weights)
        return (text_embed, split_samples(act), split_samples(base))

    def prepare_none(unused_arg):
        empty = jnp.zeros((samples_here, text_len, model_width), jnp.bfloat16)
        return (empty, empty, empty)

    branch_in, branch_act, branch_base = lax.switch(
        jnp.minimum(segment_kind, 2), [prepare_vision, prepare_text, prepare_none], 0
    )

    def forward_tick(tick, received, saved_in, saved_base):
        micro = tick - segment_index
        valid = (micro >= 0) & (micro < samples_here)
        slot = jnp.clip(micro, 0, samples_here - 1)

        def forward_vision_case(unused_arg):
            return (pad_rows(pick_one(branch_act, slot)), received)

        def forward_text_case(unused_arg):
            joined = join_rows(
                pick_one(branch_act, slot)[None],
                received[:image_len][None],
                pick_one(offsets, slot)[None],
            )
            return (joined.reshape(total_len, model_width), received)

        def forward_section_case(unused_arg):
            return segment_forward_with_base(received, *weights)

        def forward_last_case(unused_arg):
            return (received, base_of(received, value_full, out_full))

        def forward_idle_case(unused_arg):
            return (received, received)

        outgoing, keep_base = lax.switch(
            jnp.where(valid, segment_kind, 4),
            [
                forward_vision_case,
                forward_text_case,
                forward_section_case,
                forward_last_case,
                forward_idle_case,
            ],
            0,
        )
        saved_in = lax.dynamic_update_index_in_dim(
            saved_in, jnp.where(valid, received, pick_one(saved_in, slot)), slot, 0
        )
        saved_base = lax.dynamic_update_index_in_dim(
            saved_base, jnp.where(valid, keep_base, pick_one(saved_base, slot)), slot, 0
        )
        arriving = passed_along(outgoing, "segment", 1)
        return (arriving, saved_in, saved_base)

    def backward_tick(phase, received, saved_in, saved_base, totals):
        micro = phase - (segment_count - 1 - segment_index)
        valid = (micro >= 0) & (micro < samples_here)
        slot = jnp.clip(micro, 0, samples_here - 1)

        def backward_vision_case(unused_arg):
            unused_grad, part_down, part_up = segment_backward_saved(
                pick_one(branch_in, slot),
                pick_one(branch_base, slot),
                received[:image_len],
                *weights,
            )
            return (jnp.zeros((total_len, model_width), jnp.bfloat16), part_down, part_up)

        def backward_text_case(unused_arg):
            text_part, image_part = split_rows(
                received[None], pick_one(offsets, slot)[None], text_len
            )
            unused_grad, part_down, part_up = segment_backward_saved(
                pick_one(branch_in, slot), pick_one(branch_base, slot), text_part[0], *weights
            )
            return (pad_rows(image_part[0]), part_down, part_up)

        def backward_section_case(unused_arg):
            return segment_backward_saved(
                pick_one(saved_in, slot), pick_one(saved_base, slot), received, *weights
            )

        def backward_last_case(unused_arg):
            return segment_backward_saved(
                pick_one(saved_in, slot),
                pick_one(saved_base, slot),
                pick_one(cotangent, slot),
                *weights,
            )

        def backward_idle_case(unused_arg):
            zeros = jnp.zeros((rank_width, model_width), jnp.float32)
            return (received, zeros, zeros)

        outgoing, part_down, part_up = lax.switch(
            jnp.where(valid, segment_kind, 4),
            [
                backward_vision_case,
                backward_text_case,
                backward_section_case,
                backward_last_case,
                backward_idle_case,
            ],
            0,
        )
        totals = (totals[0] + part_down, totals[1] + part_up)
        arriving = passed_along(outgoing, "segment", -1)
        return (arriving, totals)

    empty_rows = jnp.zeros((total_len, model_width), jnp.bfloat16)
    saved_start = jnp.zeros((samples_here, total_len, model_width), jnp.bfloat16)
    totals_start = (
        jnp.zeros((rank_width, model_width), jnp.float32),
        jnp.zeros((rank_width, model_width), jnp.float32),
    )
    sweep_ticks = samples_here + segment_count - 1

    def forward_step(tick, carry):
        return forward_tick(tick, carry[0], carry[1], carry[2])

    unused_rows, saved_in, saved_base = lax.fori_loop(
        0, sweep_ticks, forward_step, (empty_rows, saved_start, saved_start)
    )

    def backward_step(tick, carry):
        return backward_tick(tick, carry[0], saved_in, saved_base, carry[1])

    unused_grad, totals = lax.fori_loop(0, sweep_ticks, backward_step, (empty_rows, totals_start))
    reduced_down, reduced_up = reduce_over_dp(totals[0], totals[1])
    return (reduced_down[None], reduced_up[None])


def solution(mesh):
    in_specs = (
        P("dp", None, None),
        P("dp", None, None),
        P("dp", None),
        P("dp"),
        P(),
        P("segment", "dp", None),
        P("segment", None, "dp"),
        P("segment", None, "dp"),
        P("segment", None, "dp"),
        P("dp", None, None),
    )
    out_specs = (P("segment", None, "dp"), P("segment", None, "dp"))
    return jax.shard_map(body, mesh=mesh, in_specs=in_specs, out_specs=out_specs, check_vma=False)
```

```python
import jax
import jax.numpy as jnp
from jax import lax
from jax.sharding import PartitionSpec as P

VIT_HEADS = 16


def as_sent(value):

    def short(part):
        return part.astype(jnp.bfloat16) if part.dtype == jnp.float32 else part

    return jax.tree.map(short, value)


def passed_along(value, axis, by):
    size = lax.axis_size(axis)
    pairs = [(i, i + by) for i in range(size) if 0 <= i + by < size]
    return lax.ppermute(value, axis, pairs)


def rms_scale(values):
    return lax.rsqrt(jnp.mean(values * values, axis=-1, keepdims=True) + 1e-06)


def segment_parts(inputs, value_full, out_full, down_full):
    widened = inputs.astype(jnp.float32)
    first_rms = rms_scale(widened)
    normed_one = (widened * first_rms).astype(jnp.bfloat16)
    valued = jnp.dot(normed_one, value_full, preferred_element_type=jnp.float32).astype(
        jnp.bfloat16
    )
    base = (widened + jnp.dot(valued, out_full, preferred_element_type=jnp.float32)).astype(
        jnp.bfloat16
    )
    base_wide = base.astype(jnp.float32)
    second_rms = rms_scale(base_wide)
    normed_two = (base_wide * second_rms).astype(jnp.bfloat16)
    before = lax.dot_general(
        normed_two, down_full, (((1,), (1,)), ((), ())), preferred_element_type=jnp.float32
    )
    return (widened, first_rms, base_wide, second_rms, normed_two, before)


def segment_forward(inputs, value_full, out_full, down_full, up_full):
    widened, first_rms, base_wide, second_rms, normed_two, before = segment_parts(
        inputs, value_full, out_full, down_full
    )
    hidden = jax.nn.silu(before).astype(jnp.bfloat16)
    return (base_wide + jnp.dot(hidden, up_full, preferred_element_type=jnp.float32)).astype(
        jnp.bfloat16
    )


def norm_back(grad_normed, widened, inverse_rms, upstream_wide):
    inner_mean = jnp.mean(grad_normed * widened, axis=-1, keepdims=True)
    cubed = inverse_rms * inverse_rms * inverse_rms
    return (upstream_wide + inverse_rms * grad_normed - widened * cubed * inner_mean).astype(
        jnp.bfloat16
    )


def transposed_dot(left, right):
    return lax.dot_general(
        left, right, (((1,), (1,)), ((), ())), preferred_element_type=jnp.float32
    )


def segment_backward(inputs, upstream, value_full, out_full, down_full, up_full):
    widened, first_rms, base_wide, second_rms, normed_two, before = segment_parts(
        inputs, value_full, out_full, down_full
    )
    hidden = jax.nn.silu(before).astype(jnp.bfloat16)
    up_term = lax.dot_general(
        hidden, upstream, (((0,), (0,)), ((), ())), preferred_element_type=jnp.float32
    )
    through = transposed_dot(upstream, up_full)
    sigmoid_part = jax.nn.sigmoid(before)
    grad_before = (through * sigmoid_part * (1.0 + before * (1.0 - sigmoid_part))).astype(
        jnp.bfloat16
    )
    down_term = lax.dot_general(
        grad_before, normed_two, (((0,), (0,)), ((), ())), preferred_element_type=jnp.float32
    )
    grad_two = jnp.dot(grad_before, down_full, preferred_element_type=jnp.float32)
    grad_base = norm_back(grad_two, base_wide, second_rms, upstream.astype(jnp.float32))
    grad_valued = transposed_dot(grad_base, out_full).astype(jnp.bfloat16)
    grad_one = transposed_dot(grad_valued, value_full)
    grad_inputs = norm_back(grad_one, widened, first_rms, grad_base.astype(jnp.float32))
    return (grad_inputs, down_term, up_term)


def segment_forward_with_base(inputs, value_full, out_full, down_full, up_full):
    widened, first_rms, base_wide, second_rms, normed_two, before = segment_parts(
        inputs, value_full, out_full, down_full
    )
    hidden = jax.nn.silu(before).astype(jnp.bfloat16)
    result = (base_wide + jnp.dot(hidden, up_full, preferred_element_type=jnp.float32)).astype(
        jnp.bfloat16
    )
    return result, base_wide.astype(jnp.bfloat16)


def base_of(inputs, value_full, out_full):
    widened = inputs.astype(jnp.float32)
    normed_one = (widened * rms_scale(widened)).astype(jnp.bfloat16)
    valued = jnp.dot(normed_one, value_full, preferred_element_type=jnp.float32).astype(
        jnp.bfloat16
    )
    return (widened + jnp.dot(valued, out_full, preferred_element_type=jnp.float32)).astype(
        jnp.bfloat16
    )


def segment_backward_saved(inputs, base, upstream, value_full, out_full, down_full, up_full):
    widened = inputs.astype(jnp.float32)
    first_rms = rms_scale(widened)
    base_wide = base.astype(jnp.float32)
    second_rms = rms_scale(base_wide)
    normed_two = (base_wide * second_rms).astype(jnp.bfloat16)
    before = lax.dot_general(
        normed_two, down_full, (((1,), (1,)), ((), ())), preferred_element_type=jnp.float32
    )
    hidden = jax.nn.silu(before).astype(jnp.bfloat16)
    up_term = lax.dot_general(
        hidden, upstream, (((0,), (0,)), ((), ())), preferred_element_type=jnp.float32
    )
    through = transposed_dot(upstream, up_full)
    sigmoid_part = jax.nn.sigmoid(before)
    grad_before = (through * sigmoid_part * (1.0 + before * (1.0 - sigmoid_part))).astype(
        jnp.bfloat16
    )
    down_term = lax.dot_general(
        grad_before, normed_two, (((0,), (0,)), ((), ())), preferred_element_type=jnp.float32
    )
    grad_two = jnp.dot(grad_before, down_full, preferred_element_type=jnp.float32)
    grad_base = norm_back(grad_two, base_wide, second_rms, upstream.astype(jnp.float32))
    grad_valued = transposed_dot(grad_base, out_full).astype(jnp.bfloat16)
    grad_one = transposed_dot(grad_valued, value_full)
    grad_inputs = norm_back(grad_one, widened, first_rms, grad_base.astype(jnp.float32))
    return (grad_inputs, down_term, up_term)


def vision_tokens(patch_part, id_part, vit_qkv):
    samples_here, patch_len, vision_width = patch_part.shape
    head_width = vision_width // VIT_HEADS
    widened = patch_part.astype(jnp.float32)
    normed = (widened * rms_scale(widened)).astype(jnp.bfloat16)
    projected = jnp.dot(
        normed.reshape(samples_here * patch_len, vision_width),
        vit_qkv,
        preferred_element_type=jnp.float32,
    ).astype(jnp.bfloat16)
    projected = projected.reshape(samples_here, patch_len, 3, VIT_HEADS, head_width)
    query_part = projected[:, :, 0]
    key_part = projected[:, :, 1]
    value_part = projected[:, :, 2]
    scores = jnp.einsum(
        "nqhd,nkhd->nhqk", query_part, key_part, preferred_element_type=jnp.float32
    ) * head_width ** (-0.5)
    same_window = id_part[:, None, :, None] == id_part[:, None, None, :]
    weights = jnp.where(same_window, jnp.exp(scores), 0.0)
    probabilities = (weights / jnp.sum(weights, axis=-1, keepdims=True)).astype(jnp.bfloat16)
    attended = jnp.einsum(
        "nhqk,nkhd->nqhd", probabilities, value_part, preferred_element_type=jnp.float32
    )
    vit_out = (widened + attended.reshape(samples_here, patch_len, vision_width)).astype(
        jnp.bfloat16
    )
    return vit_out.reshape(samples_here, patch_len // 4, 4 * vision_width)


def take_rows(row_block, row_index):
    return jax.vmap(lambda block_one, index_one: jnp.take(block_one, index_one, axis=0))(
        row_block, row_index
    )


def join_rows(text_rows, image_rows, offsets):
    text_len = text_rows.shape[1]
    image_len = image_rows.shape[1]
    position = jnp.arange(text_len + image_len, dtype=jnp.int32)[None, :]
    begin_at = offsets[:, None]
    in_image = (position >= begin_at) & (position < begin_at + image_len)
    text_index = jnp.clip(
        jnp.where(position < begin_at, position, position - image_len), 0, text_len - 1
    )
    image_index = jnp.clip(position - begin_at, 0, image_len - 1)
    return jnp.where(
        in_image[:, :, None], take_rows(image_rows, image_index), take_rows(text_rows, text_index)
    )


def split_rows(grad_rows, offsets, text_len):
    image_len = grad_rows.shape[1] - text_len
    begin_at = offsets[:, None]
    text_position = jnp.arange(text_len, dtype=jnp.int32)[None, :]
    text_index = jnp.where(text_position < begin_at, text_position, text_position + image_len)
    image_index = begin_at + jnp.arange(image_len, dtype=jnp.int32)[None, :]
    return (take_rows(grad_rows, text_index), take_rows(grad_rows, image_index))


def reduce_over_dp(down_total, up_total):
    parts = lax.axis_size("dp")
    both = jnp.concatenate([down_total, up_total], axis=0).astype(jnp.bfloat16)
    rows, width = both.shape
    blocks = both.reshape(rows, parts, width // parts).transpose(1, 0, 2)
    received = lax.all_to_all(blocks, "dp", 0, 0, tiled=True)
    summed = received.astype(jnp.float32).sum(axis=0)
    return summed[: down_total.shape[0]], summed[down_total.shape[0] :]


def pick_one(array, index):
    return lax.dynamic_index_in_dim(array, index, 0, keepdims=False)


def body(
    text_embed,
    patches,
    window_ids,
    offsets,
    vit_qkv,
    frozen_value,
    frozen_out,
    adapter_down,
    adapter_up,
    cotangent,
):
    segment_index = lax.axis_index("segment")
    segment_count = lax.axis_size("segment")
    samples_here, text_len, model_width = text_embed.shape
    image_len = patches.shape[1] // 4
    total_len = text_len + image_len
    value_width = frozen_value.shape[2]
    rank = adapter_down.shape[1]
    packed = jnp.concatenate(
        [frozen_value[0].T, frozen_out[0], adapter_down[0], adapter_up[0]], axis=0
    )
    gathered = lax.all_gather(packed, "dp", axis=1, tiled=True)
    value_full = gathered[:value_width].T
    out_full = gathered[value_width : 2 * value_width]
    down_full = gathered[2 * value_width : 2 * value_width + rank]
    up_full = gathered[2 * value_width + rank :]
    rank_width = down_full.shape[0]
    segment_kind = jnp.where(
        segment_index == 0,
        0,
        jnp.where(segment_index == 1, 1, jnp.where(segment_index == segment_count - 1, 3, 2)),
    )

    weights = (value_full, out_full, down_full, up_full)
    branch_rows = samples_here * text_len

    def pad_rows(rows):
        filler = jnp.zeros((total_len - rows.shape[0], model_width), rows.dtype)
        return jnp.concatenate([rows, filler], axis=0)

    def split_samples(rows):
        return rows.reshape(samples_here, rows.shape[0] // samples_here, model_width)

    def vision_only(unused_arg):
        return vision_tokens(patches, window_ids, vit_qkv)

    def no_vision(unused_arg):
        return jnp.zeros((samples_here, image_len, model_width), jnp.bfloat16)

    image_tokens = lax.cond(segment_index == 0, vision_only, no_vision, 0)

    def prepare_vision(unused_arg):
        tokens = image_tokens.reshape(samples_here * image_len, model_width)
        act, base = segment_forward_with_base(tokens, *weights)
        return (image_tokens, split_samples(act), split_samples(base))

    def prepare_text(unused_arg):
        rows = text_embed.reshape(branch_rows, model_width)
        act, base = segment_forward_with_base(rows, *weights)
        return (text_embed, split_samples(act), split_samples(base))

    def prepare_none(unused_arg):
        empty = jnp.zeros((samples_here, text_len, model_width), jnp.bfloat16)
        return (empty, empty, empty)

    branch_in, branch_act, branch_base = lax.switch(
        jnp.minimum(segment_kind, 2), [prepare_vision, prepare_text, prepare_none], 0
    )

    def merged_tick(tick, fwd_received, bwd_received, saved_in, saved_base, totals):
        micro = tick - segment_index
        valid = (micro >= 0) & (micro < samples_here)
        slot = jnp.clip(micro, 0, samples_here - 1)

        def forward_vision_case(unused_arg):
            return (pad_rows(pick_one(branch_act, slot)), fwd_received)

        def forward_text_case(unused_arg):
            joined = join_rows(
                pick_one(branch_act, slot)[None],
                fwd_received[:image_len][None],
                pick_one(offsets, slot)[None],
            )
            return (joined.reshape(total_len, model_width), fwd_received)

        def forward_section_case(unused_arg):
            return segment_forward_with_base(fwd_received, *weights)

        def forward_idle_case(unused_arg):
            return (fwd_received, fwd_received)

        fwd_kind = jnp.where(valid & (segment_kind < 3), segment_kind, 3)
        fwd_outgoing, keep_base = lax.switch(
            fwd_kind,
            [forward_vision_case, forward_text_case, forward_section_case, forward_idle_case],
            0,
        )
        keep = valid & (segment_kind == 2)
        saved_in = lax.dynamic_update_index_in_dim(
            saved_in, jnp.where(keep, fwd_received, pick_one(saved_in, slot)), slot, 0
        )
        saved_base = lax.dynamic_update_index_in_dim(
            saved_base, jnp.where(keep, keep_base, pick_one(saved_base, slot)), slot, 0
        )

        back_micro = tick - (2 * (segment_count - 1) - segment_index)
        back_valid = (back_micro >= 0) & (back_micro < samples_here)
        back_slot = jnp.clip(back_micro, 0, samples_here - 1)

        def backward_vision_case(unused_arg):
            unused_grad, part_down, part_up = segment_backward_saved(
                pick_one(branch_in, back_slot),
                pick_one(branch_base, back_slot),
                bwd_received[:image_len],
                *weights,
            )
            return (jnp.zeros((total_len, model_width), jnp.bfloat16), part_down, part_up)

        def backward_text_case(unused_arg):
            text_part, image_part = split_rows(
                bwd_received[None], pick_one(offsets, back_slot)[None], text_len
            )
            unused_grad, part_down, part_up = segment_backward_saved(
                pick_one(branch_in, back_slot),
                pick_one(branch_base, back_slot),
                text_part[0],
                *weights,
            )
            return (pad_rows(image_part[0]), part_down, part_up)

        def backward_section_case(unused_arg):
            return segment_backward_saved(
                pick_one(saved_in, back_slot),
                pick_one(saved_base, back_slot),
                bwd_received,
                *weights,
            )

        def backward_last_case(unused_arg):
            return segment_backward(
                fwd_received, pick_one(cotangent, back_slot), *weights
            )

        def backward_idle_case(unused_arg):
            zeros = jnp.zeros((rank_width, model_width), jnp.float32)
            return (bwd_received, zeros, zeros)

        bwd_outgoing, part_down, part_up = lax.switch(
            jnp.where(back_valid, segment_kind, 4),
            [
                backward_vision_case,
                backward_text_case,
                backward_section_case,
                backward_last_case,
                backward_idle_case,
            ],
            0,
        )
        totals = (totals[0] + part_down, totals[1] + part_up)
        fwd_arriving = passed_along(fwd_outgoing, "segment", 1)
        bwd_arriving = passed_along(bwd_outgoing, "segment", -1)
        return (fwd_arriving, bwd_arriving, saved_in, saved_base, totals)

    empty_rows = jnp.zeros((total_len, model_width), jnp.bfloat16)
    saved_start = jnp.zeros((samples_here, total_len, model_width), jnp.bfloat16)
    totals_start = (
        jnp.zeros((rank_width, model_width), jnp.float32),
        jnp.zeros((rank_width, model_width), jnp.float32),
    )
    sweep_ticks = samples_here + 2 * (segment_count - 1)

    def merged_step(tick, carry):
        return merged_tick(tick, *carry)

    carry = lax.fori_loop(
        0,
        sweep_ticks,
        merged_step,
        (empty_rows, empty_rows, saved_start, saved_start, totals_start),
    )
    totals = carry[4]
    reduced_down, reduced_up = reduce_over_dp(totals[0], totals[1])
    return (reduced_down[None], reduced_up[None])


def solution(mesh):
    in_specs = (
        P("dp", None, None),
        P("dp", None, None),
        P("dp", None),
        P("dp"),
        P(),
        P("segment", "dp", None),
        P("segment", None, "dp"),
        P("segment", None, "dp"),
        P("segment", None, "dp"),
        P("dp", None, None),
    )
    out_specs = (P("segment", None, "dp"), P("segment", None, "dp"))
    return jax.shard_map(body, mesh=mesh, in_specs=in_specs, out_specs=out_specs, check_vma=False)
```

```python
import jax
import jax.numpy as jnp
from jax import lax
from jax.sharding import PartitionSpec as P

VIT_HEADS = 16


def passed_along(value, axis, by):
    size = lax.axis_size(axis)
    pairs = [(i, i + by) for i in range(size) if 0 <= i + by < size]
    return lax.ppermute(value, axis, pairs)


def rms_scale(values):
    return lax.rsqrt(jnp.mean(values * values, axis=-1, keepdims=True) + 1e-06)


def segment_parts(inputs, value_full, out_full, down_full):
    widened = inputs.astype(jnp.float32)
    first_rms = rms_scale(widened)
    normed_one = (widened * first_rms).astype(jnp.bfloat16)
    valued = jnp.dot(normed_one, value_full, preferred_element_type=jnp.float32).astype(
        jnp.bfloat16
    )
    base = (widened + jnp.dot(valued, out_full, preferred_element_type=jnp.float32)).astype(
        jnp.bfloat16
    )
    base_wide = base.astype(jnp.float32)
    second_rms = rms_scale(base_wide)
    normed_two = (base_wide * second_rms).astype(jnp.bfloat16)
    before = lax.dot_general(
        normed_two, down_full, (((1,), (1,)), ((), ())), preferred_element_type=jnp.float32
    )
    return (widened, first_rms, base_wide, second_rms, normed_two, before)


def norm_back(grad_normed, widened, inverse_rms, upstream_wide):
    inner_mean = jnp.mean(grad_normed * widened, axis=-1, keepdims=True)
    cubed = inverse_rms * inverse_rms * inverse_rms
    return (upstream_wide + inverse_rms * grad_normed - widened * cubed * inner_mean).astype(
        jnp.bfloat16
    )


def transposed_dot(left, right):
    return lax.dot_general(
        left, right, (((1,), (1,)), ((), ())), preferred_element_type=jnp.float32
    )


def segment_forward_with_base(inputs, value_full, out_full, down_full, up_full):
    _, _, base_wide, _, _, before = segment_parts(inputs, value_full, out_full, down_full)
    hidden = jax.nn.silu(before).astype(jnp.bfloat16)
    result = (base_wide + jnp.dot(hidden, up_full, preferred_element_type=jnp.float32)).astype(
        jnp.bfloat16
    )
    return result, base_wide.astype(jnp.bfloat16)


def base_of(inputs, value_full, out_full):
    widened = inputs.astype(jnp.float32)
    normed_one = (widened * rms_scale(widened)).astype(jnp.bfloat16)
    valued = jnp.dot(normed_one, value_full, preferred_element_type=jnp.float32).astype(
        jnp.bfloat16
    )
    return (widened + jnp.dot(valued, out_full, preferred_element_type=jnp.float32)).astype(
        jnp.bfloat16
    )


def segment_backward_saved(inputs, base, upstream, value_full, out_full, down_full, up_full):
    widened = inputs.astype(jnp.float32)
    first_rms = rms_scale(widened)
    base_wide = base.astype(jnp.float32)
    second_rms = rms_scale(base_wide)
    normed_two = (base_wide * second_rms).astype(jnp.bfloat16)
    before = lax.dot_general(
        normed_two, down_full, (((1,), (1,)), ((), ())), preferred_element_type=jnp.float32
    )
    hidden = jax.nn.silu(before).astype(jnp.bfloat16)
    up_term = lax.dot_general(
        hidden, upstream, (((0,), (0,)), ((), ())), preferred_element_type=jnp.float32
    )
    through = transposed_dot(upstream, up_full)
    sigmoid_part = jax.nn.sigmoid(before)
    grad_before = (through * sigmoid_part * (1.0 + before * (1.0 - sigmoid_part))).astype(
        jnp.bfloat16
    )
    down_term = lax.dot_general(
        grad_before, normed_two, (((0,), (0,)), ((), ())), preferred_element_type=jnp.float32
    )
    grad_two = jnp.dot(grad_before, down_full, preferred_element_type=jnp.float32)
    grad_base = norm_back(grad_two, base_wide, second_rms, upstream.astype(jnp.float32))
    grad_valued = transposed_dot(grad_base, out_full).astype(jnp.bfloat16)
    grad_one = transposed_dot(grad_valued, value_full)
    grad_inputs = norm_back(grad_one, widened, first_rms, grad_base.astype(jnp.float32))
    return (grad_inputs, down_term, up_term)


def vision_tokens(patch_part, id_part, vit_qkv):
    samples_here, patch_len, vision_width = patch_part.shape
    head_width = vision_width // VIT_HEADS
    widened = patch_part.astype(jnp.float32)
    normed = (widened * rms_scale(widened)).astype(jnp.bfloat16)
    projected = jnp.dot(
        normed.reshape(samples_here * patch_len, vision_width),
        vit_qkv,
        preferred_element_type=jnp.float32,
    ).astype(jnp.bfloat16)
    projected = projected.reshape(samples_here, patch_len, 3, VIT_HEADS, head_width)
    query_part = projected[:, :, 0]
    key_part = projected[:, :, 1]
    value_part = projected[:, :, 2]
    scores = jnp.einsum(
        "nqhd,nkhd->nhqk", query_part, key_part, preferred_element_type=jnp.float32
    ) * head_width ** (-0.5)
    same_window = id_part[:, None, :, None] == id_part[:, None, None, :]
    weights = jnp.where(same_window, jnp.exp(scores), 0.0)
    probabilities = (weights / jnp.sum(weights, axis=-1, keepdims=True)).astype(jnp.bfloat16)
    attended = jnp.einsum(
        "nhqk,nkhd->nqhd", probabilities, value_part, preferred_element_type=jnp.float32
    )
    vit_out = (widened + attended.reshape(samples_here, patch_len, vision_width)).astype(
        jnp.bfloat16
    )
    return vit_out.reshape(samples_here, patch_len // 4, 4 * vision_width)


def take_rows(row_block, row_index):
    return jax.vmap(lambda block_one, index_one: jnp.take(block_one, index_one, axis=0))(
        row_block, row_index
    )


def join_rows(text_rows, image_rows, offsets):
    text_len = text_rows.shape[1]
    image_len = image_rows.shape[1]
    position = jnp.arange(text_len + image_len, dtype=jnp.int32)[None, :]
    begin_at = offsets[:, None]
    in_image = (position >= begin_at) & (position < begin_at + image_len)
    text_index = jnp.clip(
        jnp.where(position < begin_at, position, position - image_len), 0, text_len - 1
    )
    image_index = jnp.clip(position - begin_at, 0, image_len - 1)
    return jnp.where(
        in_image[:, :, None], take_rows(image_rows, image_index), take_rows(text_rows, text_index)
    )


def split_rows(grad_rows, offsets, text_len):
    image_len = grad_rows.shape[1] - text_len
    begin_at = offsets[:, None]
    text_position = jnp.arange(text_len, dtype=jnp.int32)[None, :]
    text_index = jnp.where(text_position < begin_at, text_position, text_position + image_len)
    image_index = begin_at + jnp.arange(image_len, dtype=jnp.int32)[None, :]
    return (take_rows(grad_rows, text_index), take_rows(grad_rows, image_index))


def reduce_over_dp(down_total, up_total):
    parts = lax.axis_size("dp")
    both = jnp.concatenate([down_total, up_total], axis=0).astype(jnp.bfloat16)
    rows, width = both.shape
    blocks = both.reshape(rows, parts, width // parts).transpose(1, 0, 2)
    received = lax.all_to_all(blocks, "dp", 0, 0, tiled=True)
    summed = received.astype(jnp.float32).sum(axis=0)
    return summed[: down_total.shape[0]], summed[down_total.shape[0] :]


def pick_one(array, index):
    return lax.dynamic_index_in_dim(array, index, 0, keepdims=False)


def body(
    text_embed,
    patches,
    window_ids,
    offsets,
    vit_qkv,
    frozen_value,
    frozen_out,
    adapter_down,
    adapter_up,
    cotangent,
):
    segment_index = lax.axis_index("segment")
    segment_count = lax.axis_size("segment")
    samples_here, text_len, model_width = text_embed.shape
    image_len = patches.shape[1] // 4
    total_len = text_len + image_len
    value_width = frozen_value.shape[2]
    rank = adapter_down.shape[1]
    packed = jnp.concatenate(
        [frozen_value[0].T, frozen_out[0], adapter_down[0], adapter_up[0]], axis=0
    )
    gathered = lax.all_gather(packed, "dp", axis=1, tiled=True)
    value_full = gathered[:value_width].T
    out_full = gathered[value_width : 2 * value_width]
    down_full = gathered[2 * value_width : 2 * value_width + rank]
    up_full = gathered[2 * value_width + rank :]
    rank_width = down_full.shape[0]
    segment_kind = jnp.where(
        segment_index == 0,
        0,
        jnp.where(segment_index == 1, 1, jnp.where(segment_index == segment_count - 1, 3, 2)),
    )

    weights = (value_full, out_full, down_full, up_full)
    branch_rows = samples_here * text_len

    def split_samples(rows):
        return rows.reshape(samples_here, rows.shape[0] // samples_here, model_width)

    def vision_only(unused_arg):
        return vision_tokens(patches, window_ids, vit_qkv)

    def no_vision(unused_arg):
        return jnp.zeros((samples_here, image_len, model_width), jnp.bfloat16)

    image_tokens = lax.cond(segment_index == 0, vision_only, no_vision, 0)

    def prepare_vision(unused_arg):
        tokens = image_tokens.reshape(samples_here * image_len, model_width)
        act, base = segment_forward_with_base(tokens, *weights)
        return (image_tokens, split_samples(act), split_samples(base))

    def prepare_text(unused_arg):
        rows = text_embed.reshape(branch_rows, model_width)
        act, base = segment_forward_with_base(rows, *weights)
        return (text_embed, split_samples(act), split_samples(base))

    def prepare_none(unused_arg):
        empty = jnp.zeros((samples_here, text_len, model_width), jnp.bfloat16)
        return (empty, empty, empty)

    branch_in, branch_act, branch_base = lax.switch(
        jnp.minimum(segment_kind, 2), [prepare_vision, prepare_text, prepare_none], 0
    )

    half = total_len // 2
    half_zeros = jnp.zeros((half, model_width), jnp.bfloat16)
    rank_zeros = jnp.zeros((rank_width, model_width), jnp.float32)

    def forward_tick(tick, received, saved_in, saved_base):
        micro = tick - segment_index
        valid = (micro >= 0) & (micro < samples_here)
        slot = jnp.clip(micro, 0, samples_here - 1)
        kind = jnp.where(valid, segment_kind, 4)
        first, second = received[:half], received[half:]

        def first_vision(unused_arg):
            return (pick_one(branch_act, slot), half_zeros, half_zeros)

        def first_text(unused_arg):
            joined = join_rows(
                pick_one(branch_act, slot)[None],
                first[None],
                pick_one(offsets, slot)[None],
            ).reshape(total_len, model_width)
            return (joined[:half], half_zeros, joined[half:])

        def first_section(unused_arg):
            out, base = segment_forward_with_base(first, *weights)
            return (out, base, half_zeros)

        def first_last(unused_arg):
            return (half_zeros, base_of(first, value_full, out_full), half_zeros)

        def first_idle(unused_arg):
            return (half_zeros, half_zeros, half_zeros)

        out_first, base_first, pending = lax.switch(
            kind, [first_vision, first_text, first_section, first_last, first_idle], 0
        )
        sent_first = passed_along(out_first, "segment", 1)

        def second_plain(unused_arg):
            return (pending, half_zeros)

        def second_section(unused_arg):
            return segment_forward_with_base(second, *weights)

        def second_last(unused_arg):
            return (half_zeros, base_of(second, value_full, out_full))

        out_second, base_second = lax.switch(
            kind, [second_plain, second_plain, second_section, second_last, second_plain], 0
        )
        sent_second = passed_along(out_second, "segment", 1)
        keep_base = jnp.concatenate([base_first, base_second], axis=0)
        saved_in = lax.dynamic_update_index_in_dim(
            saved_in, jnp.where(valid, received, pick_one(saved_in, slot)), slot, 0
        )
        saved_base = lax.dynamic_update_index_in_dim(
            saved_base, jnp.where(valid, keep_base, pick_one(saved_base, slot)), slot, 0
        )
        arriving = jnp.concatenate([sent_first, sent_second], axis=0)
        return (arriving, saved_in, saved_base)

    def backward_tick(phase, received, saved_in, saved_base, totals):
        micro = phase - (segment_count - 1 - segment_index)
        valid = (micro >= 0) & (micro < samples_here)
        slot = jnp.clip(micro, 0, samples_here - 1)
        kind = jnp.where(valid, segment_kind, 4)
        inputs_here = pick_one(saved_in, slot)
        base_here = pick_one(saved_base, slot)
        upstream_here = jnp.where(segment_kind == 3, pick_one(cotangent, slot), received)

        def first_vision(unused_arg):
            _, part_down, part_up = segment_backward_saved(
                pick_one(branch_in, slot), pick_one(branch_base, slot), received[:half], *weights
            )
            return (half_zeros, part_down, part_up)

        def first_text(unused_arg):
            text_part, image_part = split_rows(
                received[None], pick_one(offsets, slot)[None], text_len
            )
            _, part_down, part_up = segment_backward_saved(
                pick_one(branch_in, slot), pick_one(branch_base, slot), text_part[0], *weights
            )
            return (image_part[0], part_down, part_up)

        def first_section(unused_arg):
            return segment_backward_saved(
                inputs_here[:half], base_here[:half], upstream_here[:half], *weights
            )

        def idle(unused_arg):
            return (half_zeros, rank_zeros, rank_zeros)

        out_first, down_first, up_first = lax.switch(
            kind, [first_vision, first_text, first_section, first_section, idle], 0
        )
        sent_first = passed_along(out_first, "segment", -1)

        def second_section(unused_arg):
            return segment_backward_saved(
                inputs_here[half:], base_here[half:], upstream_here[half:], *weights
            )

        out_second, down_second, up_second = lax.switch(
            kind, [idle, idle, second_section, second_section, idle], 0
        )
        sent_second = passed_along(out_second, "segment", -1)
        totals = (
            totals[0] + (down_first + down_second),
            totals[1] + (up_first + up_second),
        )
        arriving = jnp.concatenate([sent_first, sent_second], axis=0)
        return (arriving, totals)

    empty_rows = jnp.zeros((total_len, model_width), jnp.bfloat16)
    saved_start = jnp.zeros((samples_here, total_len, model_width), jnp.bfloat16)
    totals_start = (
        jnp.zeros((rank_width, model_width), jnp.float32),
        jnp.zeros((rank_width, model_width), jnp.float32),
    )
    sweep_ticks = samples_here + segment_count - 1

    def forward_step(tick, carry):
        return forward_tick(tick, carry[0], carry[1], carry[2])

    _, saved_in, saved_base = lax.fori_loop(
        0, sweep_ticks, forward_step, (empty_rows, saved_start, saved_start)
    )

    def backward_step(tick, carry):
        return backward_tick(tick, carry[0], saved_in, saved_base, carry[1])

    _, totals = lax.fori_loop(0, sweep_ticks, backward_step, (empty_rows, totals_start))
    reduced_down, reduced_up = reduce_over_dp(totals[0], totals[1])
    return (reduced_down[None], reduced_up[None])


def solution(mesh):
    in_specs = (
        P("dp", None, None),
        P("dp", None, None),
        P("dp", None),
        P("dp"),
        P(),
        P("segment", "dp", None),
        P("segment", None, "dp"),
        P("segment", None, "dp"),
        P("segment", None, "dp"),
        P("dp", None, None),
    )
    out_specs = (P("segment", None, "dp"), P("segment", None, "dp"))
    return jax.shard_map(body, mesh=mesh, in_specs=in_specs, out_specs=out_specs, check_vma=False)
```

```python
import jax
import jax.numpy as jnp
from jax import lax
from jax.sharding import PartitionSpec as P

VIT_HEADS = 16


def as_sent(value):

    def short(part):
        return part.astype(jnp.bfloat16) if part.dtype == jnp.float32 else part

    return jax.tree.map(short, value)


def passed_along(value, axis, by):
    size = lax.axis_size(axis)
    pairs = [(i, i + by) for i in range(size) if 0 <= i + by < size]
    return lax.ppermute(value, axis, pairs)


def rms_scale(values):
    return lax.rsqrt(jnp.mean(values * values, axis=-1, keepdims=True) + 1e-06)


def segment_parts(inputs, value_full, out_full, down_full):
    widened = inputs.astype(jnp.float32)
    first_rms = rms_scale(widened)
    normed_one = (widened * first_rms).astype(jnp.bfloat16)
    valued = lax.optimization_barrier(
        jnp.dot(normed_one, value_full, preferred_element_type=jnp.float32).astype(jnp.bfloat16)
    )
    base = (widened + jnp.dot(valued, out_full, preferred_element_type=jnp.float32)).astype(
        jnp.bfloat16
    )
    base_wide = base.astype(jnp.float32)
    second_rms = rms_scale(base_wide)
    normed_two = (base_wide * second_rms).astype(jnp.bfloat16)
    before = lax.dot_general(
        normed_two, down_full, (((1,), (1,)), ((), ())), preferred_element_type=jnp.float32
    )
    return (widened, first_rms, base_wide, second_rms, normed_two, before)


def segment_forward(inputs, value_full, out_full, down_full, up_full):
    widened, first_rms, base_wide, second_rms, normed_two, before = segment_parts(
        inputs, value_full, out_full, down_full
    )
    hidden = jax.nn.silu(before).astype(jnp.bfloat16)
    return (base_wide + jnp.dot(hidden, up_full, preferred_element_type=jnp.float32)).astype(
        jnp.bfloat16
    )


def norm_back(grad_normed, widened, inverse_rms, upstream_wide):
    inner_mean = jnp.mean(grad_normed * widened, axis=-1, keepdims=True)
    cubed = inverse_rms * inverse_rms * inverse_rms
    return (upstream_wide + inverse_rms * grad_normed - widened * cubed * inner_mean).astype(
        jnp.bfloat16
    )


def transposed_dot(left, right):
    return lax.dot_general(
        left, right, (((1,), (1,)), ((), ())), preferred_element_type=jnp.float32
    )


def segment_backward(inputs, upstream, value_full, out_full, down_full, up_full):
    widened, first_rms, base_wide, second_rms, normed_two, before = segment_parts(
        inputs, value_full, out_full, down_full
    )
    hidden = jax.nn.silu(before).astype(jnp.bfloat16)
    up_term = lax.dot_general(
        hidden, upstream, (((0,), (0,)), ((), ())), preferred_element_type=jnp.float32
    )
    through = transposed_dot(upstream, up_full)
    sigmoid_part = jax.nn.sigmoid(before)
    grad_before = (through * sigmoid_part * (1.0 + before * (1.0 - sigmoid_part))).astype(
        jnp.bfloat16
    )
    down_term = lax.dot_general(
        grad_before, normed_two, (((0,), (0,)), ((), ())), preferred_element_type=jnp.float32
    )
    grad_two = jnp.dot(grad_before, down_full, preferred_element_type=jnp.float32)
    grad_base = norm_back(grad_two, base_wide, second_rms, upstream.astype(jnp.float32))
    grad_valued = lax.optimization_barrier(
        transposed_dot(grad_base, out_full).astype(jnp.bfloat16)
    )
    grad_one = transposed_dot(grad_valued, value_full)
    grad_inputs = norm_back(grad_one, widened, first_rms, grad_base.astype(jnp.float32))
    return (grad_inputs, down_term, up_term)


def segment_forward_with_base(inputs, value_full, out_full, down_full, up_full):
    widened, first_rms, base_wide, second_rms, normed_two, before = segment_parts(
        inputs, value_full, out_full, down_full
    )
    hidden = jax.nn.silu(before).astype(jnp.bfloat16)
    result = (base_wide + jnp.dot(hidden, up_full, preferred_element_type=jnp.float32)).astype(
        jnp.bfloat16
    )
    return result, base_wide.astype(jnp.bfloat16)


def base_of(inputs, value_full, out_full):
    widened = inputs.astype(jnp.float32)
    normed_one = (widened * rms_scale(widened)).astype(jnp.bfloat16)
    valued = lax.optimization_barrier(
        jnp.dot(normed_one, value_full, preferred_element_type=jnp.float32).astype(jnp.bfloat16)
    )
    return (widened + jnp.dot(valued, out_full, preferred_element_type=jnp.float32)).astype(
        jnp.bfloat16
    )


def segment_backward_saved(inputs, base, upstream, value_full, out_full, down_full, up_full):
    widened = inputs.astype(jnp.float32)
    first_rms = rms_scale(widened)
    base_wide = base.astype(jnp.float32)
    second_rms = rms_scale(base_wide)
    normed_two = (base_wide * second_rms).astype(jnp.bfloat16)
    before = lax.dot_general(
        normed_two, down_full, (((1,), (1,)), ((), ())), preferred_element_type=jnp.float32
    )
    hidden = jax.nn.silu(before).astype(jnp.bfloat16)
    up_term = lax.dot_general(
        hidden, upstream, (((0,), (0,)), ((), ())), preferred_element_type=jnp.float32
    )
    through = transposed_dot(upstream, up_full)
    sigmoid_part = jax.nn.sigmoid(before)
    grad_before = (through * sigmoid_part * (1.0 + before * (1.0 - sigmoid_part))).astype(
        jnp.bfloat16
    )
    down_term = lax.dot_general(
        grad_before, normed_two, (((0,), (0,)), ((), ())), preferred_element_type=jnp.float32
    )
    grad_two = jnp.dot(grad_before, down_full, preferred_element_type=jnp.float32)
    grad_base = norm_back(grad_two, base_wide, second_rms, upstream.astype(jnp.float32))
    grad_valued = lax.optimization_barrier(
        transposed_dot(grad_base, out_full).astype(jnp.bfloat16)
    )
    grad_one = transposed_dot(grad_valued, value_full)
    grad_inputs = norm_back(grad_one, widened, first_rms, grad_base.astype(jnp.float32))
    return (grad_inputs, down_term, up_term)


def vision_tokens(patch_part, id_part, vit_qkv):
    samples_here, patch_len, vision_width = patch_part.shape
    head_width = vision_width // VIT_HEADS
    widened = patch_part.astype(jnp.float32)
    normed = (widened * rms_scale(widened)).astype(jnp.bfloat16)
    projected = jnp.dot(
        normed.reshape(samples_here * patch_len, vision_width),
        vit_qkv,
        preferred_element_type=jnp.float32,
    ).astype(jnp.bfloat16)
    projected = projected.reshape(samples_here, patch_len, 3, VIT_HEADS, head_width)
    query_part = projected[:, :, 0]
    key_part = projected[:, :, 1]
    value_part = projected[:, :, 2]
    scores = jnp.einsum(
        "nqhd,nkhd->nhqk", query_part, key_part, preferred_element_type=jnp.float32
    ) * head_width ** (-0.5)
    same_window = id_part[:, None, :, None] == id_part[:, None, None, :]
    weights = jnp.where(same_window, jnp.exp(scores), 0.0)
    probabilities = (weights / jnp.sum(weights, axis=-1, keepdims=True)).astype(jnp.bfloat16)
    attended = jnp.einsum(
        "nhqk,nkhd->nqhd", probabilities, value_part, preferred_element_type=jnp.float32
    )
    vit_out = (widened + attended.reshape(samples_here, patch_len, vision_width)).astype(
        jnp.bfloat16
    )
    return vit_out.reshape(samples_here, patch_len // 4, 4 * vision_width)


def take_rows(row_block, row_index):
    return jax.vmap(lambda block_one, index_one: jnp.take(block_one, index_one, axis=0))(
        row_block, row_index
    )


def join_rows(text_rows, image_rows, offsets):
    text_len = text_rows.shape[1]
    image_len = image_rows.shape[1]
    position = jnp.arange(text_len + image_len, dtype=jnp.int32)[None, :]
    begin_at = offsets[:, None]
    in_image = (position >= begin_at) & (position < begin_at + image_len)
    text_index = jnp.clip(
        jnp.where(position < begin_at, position, position - image_len), 0, text_len - 1
    )
    image_index = jnp.clip(position - begin_at, 0, image_len - 1)
    return jnp.where(
        in_image[:, :, None], take_rows(image_rows, image_index), take_rows(text_rows, text_index)
    )


def split_rows(grad_rows, offsets, text_len):
    image_len = grad_rows.shape[1] - text_len
    begin_at = offsets[:, None]
    text_position = jnp.arange(text_len, dtype=jnp.int32)[None, :]
    text_index = jnp.where(text_position < begin_at, text_position, text_position + image_len)
    image_index = begin_at + jnp.arange(image_len, dtype=jnp.int32)[None, :]
    return (take_rows(grad_rows, text_index), take_rows(grad_rows, image_index))


def reduce_over_dp(down_total, up_total):
    parts = lax.axis_size("dp")
    both = jnp.concatenate([down_total, up_total], axis=0).astype(jnp.bfloat16)
    rows, width = both.shape
    blocks = both.reshape(rows, parts, width // parts).transpose(1, 0, 2)
    received = lax.all_to_all(blocks, "dp", 0, 0, tiled=True)
    summed = received.astype(jnp.float32).sum(axis=0)
    return summed[: down_total.shape[0]], summed[down_total.shape[0] :]


def pick_one(array, index):
    return lax.dynamic_index_in_dim(array, index, 0, keepdims=False)


def body(
    text_embed,
    patches,
    window_ids,
    offsets,
    vit_qkv,
    frozen_value,
    frozen_out,
    adapter_down,
    adapter_up,
    cotangent,
):
    segment_index = lax.axis_index("segment")
    segment_count = lax.axis_size("segment")
    samples_here, text_len, model_width = text_embed.shape
    image_len = patches.shape[1] // 4
    total_len = text_len + image_len
    value_width = frozen_value.shape[2]
    rank = adapter_down.shape[1]
    packed = jnp.concatenate(
        [frozen_value[0].T, frozen_out[0], adapter_down[0], adapter_up[0]], axis=0
    )
    gathered = lax.all_gather(packed, "dp", axis=1, tiled=True)
    value_full = gathered[:value_width].T
    out_full = gathered[value_width : 2 * value_width]
    down_full = gathered[2 * value_width : 2 * value_width + rank]
    up_full = gathered[2 * value_width + rank :]
    rank_width = down_full.shape[0]
    segment_kind = jnp.where(
        segment_index == 0,
        0,
        jnp.where(segment_index == 1, 1, jnp.where(segment_index == segment_count - 1, 3, 2)),
    )

    weights = (value_full, out_full, down_full, up_full)
    branch_rows = samples_here * text_len

    def pad_rows(rows):
        filler = jnp.zeros((total_len - rows.shape[0], model_width), rows.dtype)
        return jnp.concatenate([rows, filler], axis=0)

    def split_samples(rows):
        return rows.reshape(samples_here, rows.shape[0] // samples_here, model_width)

    def vision_only(unused_arg):
        return vision_tokens(patches, window_ids, vit_qkv)

    def no_vision(unused_arg):
        return jnp.zeros((samples_here, image_len, model_width), jnp.bfloat16)

    image_tokens = lax.cond(segment_index == 0, vision_only, no_vision, 0)

    def prepare_vision(unused_arg):
        tokens = image_tokens.reshape(samples_here * image_len, model_width)
        act, base = segment_forward_with_base(tokens, *weights)
        return (image_tokens, split_samples(act), split_samples(base))

    def prepare_text(unused_arg):
        rows = text_embed.reshape(branch_rows, model_width)
        act, base = segment_forward_with_base(rows, *weights)
        return (text_embed, split_samples(act), split_samples(base))

    def prepare_none(unused_arg):
        empty = jnp.zeros((samples_here, text_len, model_width), jnp.bfloat16)
        return (empty, empty, empty)

    branch_in, branch_act, branch_base = lax.switch(
        jnp.minimum(segment_kind, 2), [prepare_vision, prepare_text, prepare_none], 0
    )

    def forward_tick(tick, received, saved_in, saved_base):
        micro = tick - segment_index
        valid = (micro >= 0) & (micro < samples_here)
        slot = jnp.clip(micro, 0, samples_here - 1)

        def forward_vision_case(unused_arg):
            return (pad_rows(pick_one(branch_act, slot)), received)

        def forward_text_case(unused_arg):
            joined = join_rows(
                pick_one(branch_act, slot)[None],
                received[:image_len][None],
                pick_one(offsets, slot)[None],
            )
            return (joined.reshape(total_len, model_width), received)

        def forward_section_case(unused_arg):
            return segment_forward_with_base(received, *weights)

        def forward_last_case(unused_arg):
            return (received, base_of(received, value_full, out_full))

        def forward_idle_case(unused_arg):
            return (received, received)

        outgoing, keep_base = lax.switch(
            jnp.where(valid, segment_kind, 4),
            [
                forward_vision_case,
                forward_text_case,
                forward_section_case,
                forward_last_case,
                forward_idle_case,
            ],
            0,
        )
        saved_in = lax.dynamic_update_index_in_dim(
            saved_in, jnp.where(valid, received, pick_one(saved_in, slot)), slot, 0
        )
        saved_base = lax.dynamic_update_index_in_dim(
            saved_base, jnp.where(valid, keep_base, pick_one(saved_base, slot)), slot, 0
        )
        arriving = passed_along(outgoing, "segment", 1)
        return (arriving, saved_in, saved_base)

    def backward_tick(phase, received, saved_in, saved_base, totals):
        micro = phase - (segment_count - 1 - segment_index)
        valid = (micro >= 0) & (micro < samples_here)
        slot = jnp.clip(micro, 0, samples_here - 1)

        def backward_vision_case(unused_arg):
            unused_grad, part_down, part_up = segment_backward_saved(
                pick_one(branch_in, slot),
                pick_one(branch_base, slot),
                received[:image_len],
                *weights,
            )
            return (jnp.zeros((total_len, model_width), jnp.bfloat16), part_down, part_up)

        def backward_text_case(unused_arg):
            text_part, image_part = split_rows(
                received[None], pick_one(offsets, slot)[None], text_len
            )
            unused_grad, part_down, part_up = segment_backward_saved(
                pick_one(branch_in, slot), pick_one(branch_base, slot), text_part[0], *weights
            )
            return (pad_rows(image_part[0]), part_down, part_up)

        def backward_section_case(unused_arg):
            return segment_backward_saved(
                pick_one(saved_in, slot), pick_one(saved_base, slot), received, *weights
            )

        def backward_last_case(unused_arg):
            return segment_backward_saved(
                pick_one(saved_in, slot),
                pick_one(saved_base, slot),
                pick_one(cotangent, slot),
                *weights,
            )

        def backward_idle_case(unused_arg):
            zeros = jnp.zeros((rank_width, model_width), jnp.float32)
            return (received, zeros, zeros)

        outgoing, part_down, part_up = lax.switch(
            jnp.where(valid, segment_kind, 4),
            [
                backward_vision_case,
                backward_text_case,
                backward_section_case,
                backward_last_case,
                backward_idle_case,
            ],
            0,
        )
        totals = (totals[0] + part_down, totals[1] + part_up)
        arriving = passed_along(outgoing, "segment", -1)
        return (arriving, totals)

    empty_rows = jnp.zeros((total_len, model_width), jnp.bfloat16)
    saved_start = jnp.zeros((samples_here, total_len, model_width), jnp.bfloat16)
    totals_start = (
        jnp.zeros((rank_width, model_width), jnp.float32),
        jnp.zeros((rank_width, model_width), jnp.float32),
    )
    sweep_ticks = samples_here + segment_count - 1

    def forward_step(tick, carry):
        return forward_tick(tick, carry[0], carry[1], carry[2])

    unused_rows, saved_in, saved_base = lax.fori_loop(
        0, sweep_ticks, forward_step, (empty_rows, saved_start, saved_start)
    )

    def backward_step(tick, carry):
        return backward_tick(tick, carry[0], saved_in, saved_base, carry[1])

    unused_grad, totals = lax.fori_loop(0, sweep_ticks, backward_step, (empty_rows, totals_start))
    reduced_down, reduced_up = reduce_over_dp(totals[0], totals[1])
    return (reduced_down[None], reduced_up[None])


def solution(mesh):
    in_specs = (
        P("dp", None, None),
        P("dp", None, None),
        P("dp", None),
        P("dp"),
        P(),
        P("segment", "dp", None),
        P("segment", None, "dp"),
        P("segment", None, "dp"),
        P("segment", None, "dp"),
        P("dp", None, None),
    )
    out_specs = (P("segment", None, "dp"), P("segment", None, "dp"))
    return jax.shard_map(body, mesh=mesh, in_specs=in_specs, out_specs=out_specs, check_vma=False)
```

```python
import jax
import jax.numpy as jnp
from jax import lax
from jax.sharding import PartitionSpec as P

VIT_HEADS = 16


def as_sent(value):

    def short(part):
        return part.astype(jnp.bfloat16) if part.dtype == jnp.float32 else part

    return jax.tree.map(short, value)


def passed_along(value, axis, by):
    size = lax.axis_size(axis)
    pairs = [(i, i + by) for i in range(size) if 0 <= i + by < size]
    return lax.ppermute(value, axis, pairs)


def rms_scale(values):
    return lax.rsqrt(jnp.mean(values * values, axis=-1, keepdims=True) + 1e-06)


def segment_parts(inputs, value_full, out_full, down_full):
    widened = inputs.astype(jnp.float32)
    first_rms = rms_scale(widened)
    normed_one = (widened * first_rms).astype(jnp.bfloat16)
    valued = lax.optimization_barrier(
        jnp.dot(normed_one, value_full, preferred_element_type=jnp.float32).astype(jnp.bfloat16)
    )
    base = (widened + jnp.dot(valued, out_full, preferred_element_type=jnp.float32)).astype(
        jnp.bfloat16
    )
    base_wide = base.astype(jnp.float32)
    second_rms = rms_scale(base_wide)
    normed_two = (base_wide * second_rms).astype(jnp.bfloat16)
    before = lax.dot_general(
        normed_two, down_full, (((1,), (1,)), ((), ())), preferred_element_type=jnp.float32
    )
    return (widened, first_rms, base_wide, second_rms, normed_two, before)


def segment_forward(inputs, value_full, out_full, down_full, up_full):
    widened, first_rms, base_wide, second_rms, normed_two, before = segment_parts(
        inputs, value_full, out_full, down_full
    )
    hidden = jax.nn.silu(before).astype(jnp.bfloat16)
    return (base_wide + jnp.dot(hidden, up_full, preferred_element_type=jnp.float32)).astype(
        jnp.bfloat16
    )


def norm_back(grad_normed, widened, inverse_rms, upstream_wide):
    inner_mean = jnp.mean(grad_normed * widened, axis=-1, keepdims=True)
    cubed = inverse_rms * inverse_rms * inverse_rms
    return (upstream_wide + inverse_rms * grad_normed - widened * cubed * inner_mean).astype(
        jnp.bfloat16
    )


def transposed_dot(left, right):
    return lax.dot_general(
        left, right, (((1,), (1,)), ((), ())), preferred_element_type=jnp.float32
    )


def segment_backward(inputs, upstream, value_full, out_full, down_full, up_full):
    widened, first_rms, base_wide, second_rms, normed_two, before = segment_parts(
        inputs, value_full, out_full, down_full
    )
    hidden = jax.nn.silu(before).astype(jnp.bfloat16)
    up_term = lax.dot_general(
        hidden, upstream, (((0,), (0,)), ((), ())), preferred_element_type=jnp.float32
    )
    through = transposed_dot(upstream, up_full)
    sigmoid_part = jax.nn.sigmoid(before)
    grad_before = (through * sigmoid_part * (1.0 + before * (1.0 - sigmoid_part))).astype(
        jnp.bfloat16
    )
    down_term = lax.dot_general(
        grad_before, normed_two, (((0,), (0,)), ((), ())), preferred_element_type=jnp.float32
    )
    grad_two = jnp.dot(grad_before, down_full, preferred_element_type=jnp.float32)
    grad_base = norm_back(grad_two, base_wide, second_rms, upstream.astype(jnp.float32))
    grad_valued = lax.optimization_barrier(
        transposed_dot(grad_base, out_full).astype(jnp.bfloat16)
    )
    grad_one = transposed_dot(grad_valued, value_full)
    grad_inputs = norm_back(grad_one, widened, first_rms, grad_base.astype(jnp.float32))
    return (grad_inputs, down_term, up_term)


def segment_forward_with_base(inputs, value_full, out_full, down_full, up_full):
    widened, first_rms, base_wide, second_rms, normed_two, before = segment_parts(
        inputs, value_full, out_full, down_full
    )
    hidden = jax.nn.silu(before).astype(jnp.bfloat16)
    result = (base_wide + jnp.dot(hidden, up_full, preferred_element_type=jnp.float32)).astype(
        jnp.bfloat16
    )
    return result, base_wide.astype(jnp.bfloat16)


def base_of(inputs, value_full, out_full):
    widened = inputs.astype(jnp.float32)
    normed_one = (widened * rms_scale(widened)).astype(jnp.bfloat16)
    valued = lax.optimization_barrier(
        jnp.dot(normed_one, value_full, preferred_element_type=jnp.float32).astype(jnp.bfloat16)
    )
    return (widened + jnp.dot(valued, out_full, preferred_element_type=jnp.float32)).astype(
        jnp.bfloat16
    )


def segment_backward_saved(inputs, base, upstream, value_full, out_full, down_full, up_full):
    widened = inputs.astype(jnp.float32)
    first_rms = rms_scale(widened)
    base_wide = base.astype(jnp.float32)
    second_rms = rms_scale(base_wide)
    normed_two = (base_wide * second_rms).astype(jnp.bfloat16)
    before = lax.dot_general(
        normed_two, down_full, (((1,), (1,)), ((), ())), preferred_element_type=jnp.float32
    )
    hidden = jax.nn.silu(before).astype(jnp.bfloat16)
    up_term = lax.dot_general(
        hidden, upstream, (((0,), (0,)), ((), ())), preferred_element_type=jnp.float32
    )
    through = transposed_dot(upstream, up_full)
    sigmoid_part = jax.nn.sigmoid(before)
    grad_before = (through * sigmoid_part * (1.0 + before * (1.0 - sigmoid_part))).astype(
        jnp.bfloat16
    )
    down_term = lax.dot_general(
        grad_before, normed_two, (((0,), (0,)), ((), ())), preferred_element_type=jnp.float32
    )
    grad_two = jnp.dot(grad_before, down_full, preferred_element_type=jnp.float32)
    grad_base = norm_back(grad_two, base_wide, second_rms, upstream.astype(jnp.float32))
    grad_valued = lax.optimization_barrier(
        transposed_dot(grad_base, out_full).astype(jnp.bfloat16)
    )
    grad_one = transposed_dot(grad_valued, value_full)
    grad_inputs = norm_back(grad_one, widened, first_rms, grad_base.astype(jnp.float32))
    return (grad_inputs, down_term, up_term)


def segment_backward_head(inputs, base, upstream, value_full, out_full, down_full, up_full):
    widened = inputs.astype(jnp.float32)
    first_rms = rms_scale(widened)
    base_wide = base.astype(jnp.float32)
    second_rms = rms_scale(base_wide)
    normed_two = (base_wide * second_rms).astype(jnp.bfloat16)
    before = lax.dot_general(
        normed_two, down_full, (((1,), (1,)), ((), ())), preferred_element_type=jnp.float32
    )
    hidden = jax.nn.silu(before).astype(jnp.bfloat16)
    through = transposed_dot(upstream, up_full)
    sigmoid_part = jax.nn.sigmoid(before)
    grad_before = (through * sigmoid_part * (1.0 + before * (1.0 - sigmoid_part))).astype(
        jnp.bfloat16
    )
    grad_two = jnp.dot(grad_before, down_full, preferred_element_type=jnp.float32)
    grad_base = norm_back(grad_two, base_wide, second_rms, upstream.astype(jnp.float32))
    grad_valued = lax.optimization_barrier(
        transposed_dot(grad_base, out_full).astype(jnp.bfloat16)
    )
    grad_one = transposed_dot(grad_valued, value_full)
    grad_inputs = norm_back(grad_one, widened, first_rms, grad_base.astype(jnp.float32))
    return (grad_inputs, hidden, grad_before, normed_two)


def vision_tokens(patch_part, id_part, vit_qkv):
    samples_here, patch_len, vision_width = patch_part.shape
    head_width = vision_width // VIT_HEADS
    widened = patch_part.astype(jnp.float32)
    normed = (widened * rms_scale(widened)).astype(jnp.bfloat16)
    projected = jnp.dot(
        normed.reshape(samples_here * patch_len, vision_width),
        vit_qkv,
        preferred_element_type=jnp.float32,
    ).astype(jnp.bfloat16)
    projected = projected.reshape(samples_here, patch_len, 3, VIT_HEADS, head_width)
    query_part = projected[:, :, 0]
    key_part = projected[:, :, 1]
    value_part = projected[:, :, 2]
    scores = jnp.einsum(
        "nqhd,nkhd->nhqk", query_part, key_part, preferred_element_type=jnp.float32
    ) * head_width ** (-0.5)
    same_window = id_part[:, None, :, None] == id_part[:, None, None, :]
    weights = jnp.where(same_window, jnp.exp(scores), 0.0)
    probabilities = (weights / jnp.sum(weights, axis=-1, keepdims=True)).astype(jnp.bfloat16)
    attended = jnp.einsum(
        "nhqk,nkhd->nqhd", probabilities, value_part, preferred_element_type=jnp.float32
    )
    vit_out = (widened + attended.reshape(samples_here, patch_len, vision_width)).astype(
        jnp.bfloat16
    )
    return vit_out.reshape(samples_here, patch_len // 4, 4 * vision_width)


def take_rows(row_block, row_index):
    return jax.vmap(lambda block_one, index_one: jnp.take(block_one, index_one, axis=0))(
        row_block, row_index
    )


def join_rows(text_rows, image_rows, offsets):
    text_len = text_rows.shape[1]
    image_len = image_rows.shape[1]
    position = jnp.arange(text_len + image_len, dtype=jnp.int32)[None, :]
    begin_at = offsets[:, None]
    in_image = (position >= begin_at) & (position < begin_at + image_len)
    text_index = jnp.clip(
        jnp.where(position < begin_at, position, position - image_len), 0, text_len - 1
    )
    image_index = jnp.clip(position - begin_at, 0, image_len - 1)
    return jnp.where(
        in_image[:, :, None], take_rows(image_rows, image_index), take_rows(text_rows, text_index)
    )


def split_rows(grad_rows, offsets, text_len):
    image_len = grad_rows.shape[1] - text_len
    begin_at = offsets[:, None]
    text_position = jnp.arange(text_len, dtype=jnp.int32)[None, :]
    text_index = jnp.where(text_position < begin_at, text_position, text_position + image_len)
    image_index = begin_at + jnp.arange(image_len, dtype=jnp.int32)[None, :]
    return (take_rows(grad_rows, text_index), take_rows(grad_rows, image_index))


def reduce_over_dp(down_total, up_total):
    parts = lax.axis_size("dp")
    both = jnp.concatenate([down_total, up_total], axis=0).astype(jnp.bfloat16)
    rows, width = both.shape
    blocks = both.reshape(rows, parts, width // parts).transpose(1, 0, 2)
    received = lax.all_to_all(blocks, "dp", 0, 0, tiled=True)
    summed = received.astype(jnp.float32).sum(axis=0)
    return summed[: down_total.shape[0]], summed[down_total.shape[0] :]


def pick_one(array, index):
    return lax.dynamic_index_in_dim(array, index, 0, keepdims=False)


def body(
    text_embed,
    patches,
    window_ids,
    offsets,
    vit_qkv,
    frozen_value,
    frozen_out,
    adapter_down,
    adapter_up,
    cotangent,
):
    segment_index = lax.axis_index("segment")
    segment_count = lax.axis_size("segment")
    samples_here, text_len, model_width = text_embed.shape
    image_len = patches.shape[1] // 4
    total_len = text_len + image_len
    value_width = frozen_value.shape[2]
    rank = adapter_down.shape[1]
    packed = jnp.concatenate(
        [frozen_value[0].T, frozen_out[0], adapter_down[0], adapter_up[0]], axis=0
    )
    gathered = lax.all_gather(packed, "dp", axis=1, tiled=True)
    value_full = gathered[:value_width].T
    out_full = gathered[value_width : 2 * value_width]
    down_full = gathered[2 * value_width : 2 * value_width + rank]
    up_full = gathered[2 * value_width + rank :]
    rank_width = down_full.shape[0]
    segment_kind = jnp.where(
        segment_index == 0,
        0,
        jnp.where(segment_index == 1, 1, jnp.where(segment_index == segment_count - 1, 3, 2)),
    )

    weights = (value_full, out_full, down_full, up_full)
    branch_rows = samples_here * text_len

    def pad_rows(rows):
        filler = jnp.zeros((total_len - rows.shape[0], model_width), rows.dtype)
        return jnp.concatenate([rows, filler], axis=0)

    def split_samples(rows):
        return rows.reshape(samples_here, rows.shape[0] // samples_here, model_width)

    def vision_only(unused_arg):
        return vision_tokens(patches, window_ids, vit_qkv)

    def no_vision(unused_arg):
        return jnp.zeros((samples_here, image_len, model_width), jnp.bfloat16)

    image_tokens = lax.cond(segment_index == 0, vision_only, no_vision, 0)

    def prepare_vision(unused_arg):
        tokens = image_tokens.reshape(samples_here * image_len, model_width)
        act, base = segment_forward_with_base(tokens, *weights)
        return (image_tokens, split_samples(act), split_samples(base))

    def prepare_text(unused_arg):
        rows = text_embed.reshape(branch_rows, model_width)
        act, base = segment_forward_with_base(rows, *weights)
        return (text_embed, split_samples(act), split_samples(base))

    def prepare_none(unused_arg):
        empty = jnp.zeros((samples_here, text_len, model_width), jnp.bfloat16)
        return (empty, empty, empty)

    branch_in, branch_act, branch_base = lax.switch(
        jnp.minimum(segment_kind, 2), [prepare_vision, prepare_text, prepare_none], 0
    )

    def forward_tick(tick, received, saved_in, saved_base):
        micro = tick - segment_index
        valid = (micro >= 0) & (micro < samples_here)
        slot = jnp.clip(micro, 0, samples_here - 1)

        def forward_vision_case(unused_arg):
            return (pad_rows(pick_one(branch_act, slot)), received)

        def forward_text_case(unused_arg):
            joined = join_rows(
                pick_one(branch_act, slot)[None],
                received[:image_len][None],
                pick_one(offsets, slot)[None],
            )
            return (joined.reshape(total_len, model_width), received)

        def forward_section_case(unused_arg):
            return segment_forward_with_base(received, *weights)

        def forward_last_case(unused_arg):
            return (received, base_of(received, value_full, out_full))

        def forward_idle_case(unused_arg):
            return (received, received)

        outgoing, keep_base = lax.switch(
            jnp.where(valid, segment_kind, 4),
            [
                forward_vision_case,
                forward_text_case,
                forward_section_case,
                forward_last_case,
                forward_idle_case,
            ],
            0,
        )
        saved_in = lax.dynamic_update_index_in_dim(
            saved_in, jnp.where(valid, received, pick_one(saved_in, slot)), slot, 0
        )
        saved_base = lax.dynamic_update_index_in_dim(
            saved_base, jnp.where(valid, keep_base, pick_one(saved_base, slot)), slot, 0
        )
        arriving = passed_along(outgoing, "segment", 1)
        return (arriving, saved_in, saved_base)

    def backward_tick(phase, received, saved_in, saved_base, totals):
        micro = phase - (segment_count - 1 - segment_index)
        valid = (micro >= 0) & (micro < samples_here)
        slot = jnp.clip(micro, 0, samples_here - 1)

        def pad_any(rows):
            filler = jnp.zeros((total_len - rows.shape[0], rows.shape[1]), rows.dtype)
            return jnp.concatenate([rows, filler], axis=0)

        def head_padded(inputs, base, upstream):
            grad_inputs, hidden, grad_before, normed_two = segment_backward_head(
                inputs, base, upstream, *weights
            )
            return (pad_any(hidden), pad_any(grad_before), pad_rows(normed_two), pad_rows(upstream))

        def backward_vision_case(unused_arg):
            upstream = received[:image_len]
            parts = head_padded(pick_one(branch_in, slot), pick_one(branch_base, slot), upstream)
            return (jnp.zeros((total_len, model_width), jnp.bfloat16),) + parts

        def backward_text_case(unused_arg):
            text_part, image_part = split_rows(
                received[None], pick_one(offsets, slot)[None], text_len
            )
            parts = head_padded(
                pick_one(branch_in, slot), pick_one(branch_base, slot), text_part[0]
            )
            return (pad_rows(image_part[0]),) + parts

        def section_common(upstream):
            grad_inputs, hidden, grad_before, normed_two = segment_backward_head(
                pick_one(saved_in, slot), pick_one(saved_base, slot), upstream, *weights
            )
            return (grad_inputs, hidden, grad_before, normed_two, upstream)

        def backward_section_case(unused_arg):
            return section_common(received)

        def backward_last_case(unused_arg):
            return section_common(pick_one(cotangent, slot))

        def backward_idle_case(unused_arg):
            small = jnp.zeros((total_len, rank_width), jnp.bfloat16)
            return (received, small, small, jnp.zeros_like(received), jnp.zeros_like(received))

        outgoing, hidden, grad_before, normed_two, upstream = lax.switch(
            jnp.where(valid, segment_kind, 4),
            [
                backward_vision_case,
                backward_text_case,
                backward_section_case,
                backward_last_case,
                backward_idle_case,
            ],
            0,
        )
        arriving = passed_along(outgoing, "segment", -1)
        up_term = lax.dot_general(
            hidden, upstream, (((0,), (0,)), ((), ())), preferred_element_type=jnp.float32
        )
        down_term = lax.dot_general(
            grad_before, normed_two, (((0,), (0,)), ((), ())), preferred_element_type=jnp.float32
        )
        totals = (totals[0] + down_term, totals[1] + up_term)
        return (arriving, totals)

    empty_rows = jnp.zeros((total_len, model_width), jnp.bfloat16)
    saved_start = jnp.zeros((samples_here, total_len, model_width), jnp.bfloat16)
    totals_start = (
        jnp.zeros((rank_width, model_width), jnp.float32),
        jnp.zeros((rank_width, model_width), jnp.float32),
    )
    sweep_ticks = samples_here + segment_count - 1

    def forward_step(tick, carry):
        return forward_tick(tick, carry[0], carry[1], carry[2])

    unused_rows, saved_in, saved_base = lax.fori_loop(
        0, sweep_ticks, forward_step, (empty_rows, saved_start, saved_start)
    )

    def backward_step(tick, carry):
        return backward_tick(tick, carry[0], saved_in, saved_base, carry[1])

    unused_grad, totals = lax.fori_loop(0, sweep_ticks, backward_step, (empty_rows, totals_start))
    reduced_down, reduced_up = reduce_over_dp(totals[0], totals[1])
    return (reduced_down[None], reduced_up[None])


def solution(mesh):
    in_specs = (
        P("dp", None, None),
        P("dp", None, None),
        P("dp", None),
        P("dp"),
        P(),
        P("segment", "dp", None),
        P("segment", None, "dp"),
        P("segment", None, "dp"),
        P("segment", None, "dp"),
        P("dp", None, None),
    )
    out_specs = (P("segment", None, "dp"), P("segment", None, "dp"))
    return jax.shard_map(body, mesh=mesh, in_specs=in_specs, out_specs=out_specs, check_vma=False)
```

```python
import jax
import jax.numpy as jnp
from jax import lax
from jax.sharding import PartitionSpec as P

VIT_HEADS = 16


def as_sent(value):

    def short(part):
        return part.astype(jnp.bfloat16) if part.dtype == jnp.float32 else part

    return jax.tree.map(short, value)


def passed_along(value, axis, by):
    size = lax.axis_size(axis)
    pairs = [(i, i + by) for i in range(size) if 0 <= i + by < size]
    return lax.ppermute(value, axis, pairs)


def rms_scale(values):
    return lax.rsqrt(jnp.mean(values * values, axis=-1, keepdims=True) + 1e-06)


def segment_parts(inputs, value_full, out_full, down_full):
    widened = inputs.astype(jnp.float32)
    first_rms = rms_scale(widened)
    normed_one = (widened * first_rms).astype(jnp.bfloat16)
    valued = lax.optimization_barrier(
        jnp.dot(normed_one, value_full, preferred_element_type=jnp.float32).astype(jnp.bfloat16)
    )
    base = (widened + jnp.dot(valued, out_full, preferred_element_type=jnp.float32)).astype(
        jnp.bfloat16
    )
    base_wide = base.astype(jnp.float32)
    second_rms = rms_scale(base_wide)
    normed_two = (base_wide * second_rms).astype(jnp.bfloat16)
    before = lax.dot_general(
        normed_two, down_full, (((1,), (1,)), ((), ())), preferred_element_type=jnp.float32
    )
    return (widened, first_rms, base_wide, second_rms, normed_two, before)


def segment_forward(inputs, value_full, out_full, down_full, up_full):
    widened, first_rms, base_wide, second_rms, normed_two, before = segment_parts(
        inputs, value_full, out_full, down_full
    )
    hidden = jax.nn.silu(before).astype(jnp.bfloat16)
    return (base_wide + jnp.dot(hidden, up_full, preferred_element_type=jnp.float32)).astype(
        jnp.bfloat16
    )


def norm_back(grad_normed, widened, inverse_rms, upstream_wide):
    inner_mean = jnp.mean(grad_normed * widened, axis=-1, keepdims=True)
    cubed = inverse_rms * inverse_rms * inverse_rms
    return (upstream_wide + inverse_rms * grad_normed - widened * cubed * inner_mean).astype(
        jnp.bfloat16
    )


def transposed_dot(left, right):
    return lax.dot_general(
        left, right, (((1,), (1,)), ((), ())), preferred_element_type=jnp.float32
    )


def segment_backward(inputs, upstream, value_full, out_full, down_full, up_full):
    widened, first_rms, base_wide, second_rms, normed_two, before = segment_parts(
        inputs, value_full, out_full, down_full
    )
    hidden = jax.nn.silu(before).astype(jnp.bfloat16)
    up_term = lax.dot_general(
        hidden, upstream, (((0,), (0,)), ((), ())), preferred_element_type=jnp.float32
    )
    through = transposed_dot(upstream, up_full)
    sigmoid_part = jax.nn.sigmoid(before)
    grad_before = (through * sigmoid_part * (1.0 + before * (1.0 - sigmoid_part))).astype(
        jnp.bfloat16
    )
    down_term = lax.dot_general(
        grad_before, normed_two, (((0,), (0,)), ((), ())), preferred_element_type=jnp.float32
    )
    grad_two = jnp.dot(grad_before, down_full, preferred_element_type=jnp.float32)
    grad_base = norm_back(grad_two, base_wide, second_rms, upstream.astype(jnp.float32))
    grad_valued = lax.optimization_barrier(
        transposed_dot(grad_base, out_full).astype(jnp.bfloat16)
    )
    grad_one = transposed_dot(grad_valued, value_full)
    grad_inputs = norm_back(grad_one, widened, first_rms, grad_base.astype(jnp.float32))
    return (grad_inputs, down_term, up_term)


def segment_forward_with_base(inputs, value_full, out_full, down_full, up_full):
    widened, first_rms, base_wide, second_rms, normed_two, before = segment_parts(
        inputs, value_full, out_full, down_full
    )
    hidden = jax.nn.silu(before).astype(jnp.bfloat16)
    result = (base_wide + jnp.dot(hidden, up_full, preferred_element_type=jnp.float32)).astype(
        jnp.bfloat16
    )
    return result, base_wide.astype(jnp.bfloat16)


def base_of(inputs, value_full, out_full):
    widened = inputs.astype(jnp.float32)
    normed_one = (widened * rms_scale(widened)).astype(jnp.bfloat16)
    valued = lax.optimization_barrier(
        jnp.dot(normed_one, value_full, preferred_element_type=jnp.float32).astype(jnp.bfloat16)
    )
    return (widened + jnp.dot(valued, out_full, preferred_element_type=jnp.float32)).astype(
        jnp.bfloat16
    )


def segment_backward_saved(inputs, base, upstream, value_full, out_full, down_full, up_full):
    widened = inputs.astype(jnp.float32)
    first_rms = rms_scale(widened)
    base_wide = base.astype(jnp.float32)
    second_rms = rms_scale(base_wide)
    normed_two = (base_wide * second_rms).astype(jnp.bfloat16)
    before = lax.dot_general(
        normed_two, down_full, (((1,), (1,)), ((), ())), preferred_element_type=jnp.float32
    )
    hidden = jax.nn.silu(before).astype(jnp.bfloat16)
    up_term = lax.dot_general(
        hidden, upstream, (((0,), (0,)), ((), ())), preferred_element_type=jnp.float32
    )
    through = transposed_dot(upstream, up_full)
    sigmoid_part = jax.nn.sigmoid(before)
    grad_before = (through * sigmoid_part * (1.0 + before * (1.0 - sigmoid_part))).astype(
        jnp.bfloat16
    )
    down_term = lax.dot_general(
        grad_before, normed_two, (((0,), (0,)), ((), ())), preferred_element_type=jnp.float32
    )
    grad_two = jnp.dot(grad_before, down_full, preferred_element_type=jnp.float32)
    grad_base = norm_back(grad_two, base_wide, second_rms, upstream.astype(jnp.float32))
    grad_valued = lax.optimization_barrier(
        transposed_dot(grad_base, out_full).astype(jnp.bfloat16)
    )
    grad_one = transposed_dot(grad_valued, value_full)
    grad_inputs = norm_back(grad_one, widened, first_rms, grad_base.astype(jnp.float32))
    return (grad_inputs, down_term, up_term)


def segment_backward_head(inputs, base, upstream, value_full, out_full, down_full, up_full):
    widened = inputs.astype(jnp.float32)
    first_rms = rms_scale(widened)
    base_wide = base.astype(jnp.float32)
    second_rms = rms_scale(base_wide)
    normed_two = (base_wide * second_rms).astype(jnp.bfloat16)
    before = lax.dot_general(
        normed_two, down_full, (((1,), (1,)), ((), ())), preferred_element_type=jnp.float32
    )
    hidden = jax.nn.silu(before).astype(jnp.bfloat16)
    through = transposed_dot(upstream, up_full)
    sigmoid_part = jax.nn.sigmoid(before)
    grad_before = (through * sigmoid_part * (1.0 + before * (1.0 - sigmoid_part))).astype(
        jnp.bfloat16
    )
    grad_two = jnp.dot(grad_before, down_full, preferred_element_type=jnp.float32)
    grad_base = norm_back(grad_two, base_wide, second_rms, upstream.astype(jnp.float32))
    grad_valued = lax.optimization_barrier(
        transposed_dot(grad_base, out_full).astype(jnp.bfloat16)
    )
    grad_one = transposed_dot(grad_valued, value_full)
    grad_inputs = norm_back(grad_one, widened, first_rms, grad_base.astype(jnp.float32))
    return (grad_inputs, hidden, grad_before, normed_two)


def vision_tokens(patch_part, id_part, vit_qkv):
    samples_here, patch_len, vision_width = patch_part.shape
    head_width = vision_width // VIT_HEADS
    widened = patch_part.astype(jnp.float32)
    normed = (widened * rms_scale(widened)).astype(jnp.bfloat16)
    projected = jnp.dot(
        normed.reshape(samples_here * patch_len, vision_width),
        vit_qkv,
        preferred_element_type=jnp.float32,
    ).astype(jnp.bfloat16)
    projected = projected.reshape(samples_here, patch_len, 3, VIT_HEADS, head_width)
    query_part = projected[:, :, 0]
    key_part = projected[:, :, 1]
    value_part = projected[:, :, 2]
    scores = jnp.einsum(
        "nqhd,nkhd->nhqk", query_part, key_part, preferred_element_type=jnp.float32
    ) * head_width ** (-0.5)
    same_window = id_part[:, None, :, None] == id_part[:, None, None, :]
    weights = jnp.where(same_window, jnp.exp(scores), 0.0)
    probabilities = (weights / jnp.sum(weights, axis=-1, keepdims=True)).astype(jnp.bfloat16)
    attended = jnp.einsum(
        "nhqk,nkhd->nqhd", probabilities, value_part, preferred_element_type=jnp.float32
    )
    vit_out = (widened + attended.reshape(samples_here, patch_len, vision_width)).astype(
        jnp.bfloat16
    )
    return vit_out.reshape(samples_here, patch_len // 4, 4 * vision_width)


def take_rows(row_block, row_index):
    return jax.vmap(lambda block_one, index_one: jnp.take(block_one, index_one, axis=0))(
        row_block, row_index
    )


def join_rows(text_rows, image_rows, offsets):
    text_len = text_rows.shape[1]
    image_len = image_rows.shape[1]
    position = jnp.arange(text_len + image_len, dtype=jnp.int32)[None, :]
    begin_at = offsets[:, None]
    in_image = (position >= begin_at) & (position < begin_at + image_len)
    text_index = jnp.clip(
        jnp.where(position < begin_at, position, position - image_len), 0, text_len - 1
    )
    image_index = jnp.clip(position - begin_at, 0, image_len - 1)
    return jnp.where(
        in_image[:, :, None], take_rows(image_rows, image_index), take_rows(text_rows, text_index)
    )


def split_rows(grad_rows, offsets, text_len):
    image_len = grad_rows.shape[1] - text_len
    begin_at = offsets[:, None]
    text_position = jnp.arange(text_len, dtype=jnp.int32)[None, :]
    text_index = jnp.where(text_position < begin_at, text_position, text_position + image_len)
    image_index = begin_at + jnp.arange(image_len, dtype=jnp.int32)[None, :]
    return (take_rows(grad_rows, text_index), take_rows(grad_rows, image_index))


def reduce_over_dp(down_total, up_total):
    parts = lax.axis_size("dp")
    both = jnp.concatenate([down_total, up_total], axis=0).astype(jnp.bfloat16)
    rows, width = both.shape
    blocks = both.reshape(rows, parts, width // parts).transpose(1, 0, 2)
    received = lax.all_to_all(blocks, "dp", 0, 0, tiled=True)
    summed = received.astype(jnp.float32).sum(axis=0)
    return summed[: down_total.shape[0]], summed[down_total.shape[0] :]


def pick_one(array, index):
    return lax.dynamic_index_in_dim(array, index, 0, keepdims=False)


def body(
    text_embed,
    patches,
    window_ids,
    offsets,
    vit_qkv,
    frozen_value,
    frozen_out,
    adapter_down,
    adapter_up,
    cotangent,
):
    segment_index = lax.axis_index("segment")
    segment_count = lax.axis_size("segment")
    samples_here, text_len, model_width = text_embed.shape
    image_len = patches.shape[1] // 4
    total_len = text_len + image_len
    value_width = frozen_value.shape[2]
    rank = adapter_down.shape[1]
    packed = jnp.concatenate(
        [frozen_value[0].T, frozen_out[0], adapter_down[0], adapter_up[0]], axis=0
    )
    gathered = lax.all_gather(packed, "dp", axis=1, tiled=True)
    value_full = gathered[:value_width].T
    out_full = gathered[value_width : 2 * value_width]
    down_full = gathered[2 * value_width : 2 * value_width + rank]
    up_full = gathered[2 * value_width + rank :]
    rank_width = down_full.shape[0]
    segment_kind = jnp.where(
        segment_index == 0,
        0,
        jnp.where(segment_index == 1, 1, jnp.where(segment_index == segment_count - 1, 3, 2)),
    )

    weights = (value_full, out_full, down_full, up_full)
    branch_rows = samples_here * text_len

    def pad_rows(rows):
        filler = jnp.zeros((total_len - rows.shape[0], model_width), rows.dtype)
        return jnp.concatenate([rows, filler], axis=0)

    def split_samples(rows):
        return rows.reshape(samples_here, rows.shape[0] // samples_here, model_width)

    def vision_only(unused_arg):
        return vision_tokens(patches, window_ids, vit_qkv)

    def no_vision(unused_arg):
        return jnp.zeros((samples_here, image_len, model_width), jnp.bfloat16)

    image_tokens = lax.cond(segment_index == 0, vision_only, no_vision, 0)

    def prepare_vision(unused_arg):
        tokens = image_tokens.reshape(samples_here * image_len, model_width)
        act, base = segment_forward_with_base(tokens, *weights)
        return (image_tokens, split_samples(act), split_samples(base))

    def prepare_text(unused_arg):
        rows = text_embed.reshape(branch_rows, model_width)
        act, base = segment_forward_with_base(rows, *weights)
        return (text_embed, split_samples(act), split_samples(base))

    def prepare_none(unused_arg):
        empty = jnp.zeros((samples_here, text_len, model_width), jnp.bfloat16)
        return (empty, empty, empty)

    branch_in, branch_act, branch_base = lax.switch(
        jnp.minimum(segment_kind, 2), [prepare_vision, prepare_text, prepare_none], 0
    )

    def forward_tick(tick, received, saved_in, saved_base):
        micro = tick - segment_index
        valid = (micro >= 0) & (micro < samples_here)
        slot = jnp.clip(micro, 0, samples_here - 1)

        def forward_vision_case(unused_arg):
            return (pad_rows(pick_one(branch_act, slot)), received)

        def forward_text_case(unused_arg):
            joined = join_rows(
                pick_one(branch_act, slot)[None],
                received[:image_len][None],
                pick_one(offsets, slot)[None],
            )
            return (joined.reshape(total_len, model_width), received)

        def forward_section_case(unused_arg):
            return segment_forward_with_base(received, *weights)

        def forward_last_case(unused_arg):
            return (received, base_of(received, value_full, out_full))

        def forward_idle_case(unused_arg):
            return (received, received)

        outgoing, keep_base = lax.switch(
            jnp.where(valid, segment_kind, 4),
            [
                forward_vision_case,
                forward_text_case,
                forward_section_case,
                forward_last_case,
                forward_idle_case,
            ],
            0,
        )
        saved_in = lax.dynamic_update_index_in_dim(
            saved_in, jnp.where(valid, received, pick_one(saved_in, slot)), slot, 0
        )
        saved_base = lax.dynamic_update_index_in_dim(
            saved_base, jnp.where(valid, keep_base, pick_one(saved_base, slot)), slot, 0
        )
        arriving = passed_along(outgoing, "segment", 1)
        return (arriving, saved_in, saved_base)

    def backward_tick(phase, received, saved_in, saved_base, totals):
        micro = phase - (segment_count - 1 - segment_index)
        valid = (micro >= 0) & (micro < samples_here)
        slot = jnp.clip(micro, 0, samples_here - 1)

        def pad_any(rows):
            filler = jnp.zeros((total_len - rows.shape[0], rows.shape[1]), rows.dtype)
            return jnp.concatenate([rows, filler], axis=0)

        def head_padded(inputs, base, upstream):
            grad_inputs, hidden, grad_before, normed_two = segment_backward_head(
                inputs, base, upstream, *weights
            )
            return (pad_any(hidden), pad_any(grad_before), pad_rows(normed_two), pad_rows(upstream))

        small_zeros = jnp.zeros((total_len, rank_width), jnp.bfloat16)
        wide_zeros = jnp.zeros((total_len, model_width), jnp.bfloat16)

        def backward_vision_case(unused_arg):
            return (wide_zeros, small_zeros, small_zeros, wide_zeros, received)

        def backward_text_case(unused_arg):
            text_part, image_part = split_rows(
                received[None], pick_one(offsets, slot)[None], text_len
            )
            return (pad_rows(image_part[0]), small_zeros, small_zeros, wide_zeros, pad_rows(text_part[0]))

        def section_common(upstream):
            grad_inputs, hidden, grad_before, normed_two = segment_backward_head(
                pick_one(saved_in, slot), pick_one(saved_base, slot), upstream, *weights
            )
            return (grad_inputs, hidden, grad_before, normed_two, upstream)

        def backward_section_case(unused_arg):
            return section_common(received)

        def backward_last_case(unused_arg):
            return section_common(pick_one(cotangent, slot))

        def backward_idle_case(unused_arg):
            return (received, small_zeros, small_zeros, jnp.zeros_like(received), jnp.zeros_like(received))

        outgoing, hidden, grad_before, normed_two, upstream = lax.switch(
            jnp.where(valid, segment_kind, 4),
            [
                backward_vision_case,
                backward_text_case,
                backward_section_case,
                backward_last_case,
                backward_idle_case,
            ],
            0,
        )
        arriving = passed_along(outgoing, "segment", -1)

        def branch_head(unused_arg):
            return head_padded(pick_one(branch_in, slot), pick_one(branch_base, slot), upstream[:text_len])

        def branch_pass(unused_arg):
            return (hidden, grad_before, normed_two, upstream)

        hidden, grad_before, normed_two, upstream = lax.switch(
            jnp.where(valid & (segment_kind < 2), 0, 1), [branch_head, branch_pass], 0
        )
        up_term = lax.dot_general(
            hidden, upstream, (((0,), (0,)), ((), ())), preferred_element_type=jnp.float32
        )
        down_term = lax.dot_general(
            grad_before, normed_two, (((0,), (0,)), ((), ())), preferred_element_type=jnp.float32
        )
        totals = (totals[0] + down_term, totals[1] + up_term)
        return (arriving, totals)

    empty_rows = jnp.zeros((total_len, model_width), jnp.bfloat16)
    saved_start = jnp.zeros((samples_here, total_len, model_width), jnp.bfloat16)
    totals_start = (
        jnp.zeros((rank_width, model_width), jnp.float32),
        jnp.zeros((rank_width, model_width), jnp.float32),
    )
    sweep_ticks = samples_here + segment_count - 1

    def forward_step(tick, carry):
        return forward_tick(tick, carry[0], carry[1], carry[2])

    unused_rows, saved_in, saved_base = lax.fori_loop(
        0, sweep_ticks, forward_step, (empty_rows, saved_start, saved_start)
    )

    def backward_step(tick, carry):
        return backward_tick(tick, carry[0], saved_in, saved_base, carry[1])

    unused_grad, totals = lax.fori_loop(0, sweep_ticks, backward_step, (empty_rows, totals_start))
    reduced_down, reduced_up = reduce_over_dp(totals[0], totals[1])
    return (reduced_down[None], reduced_up[None])


def solution(mesh):
    in_specs = (
        P("dp", None, None),
        P("dp", None, None),
        P("dp", None),
        P("dp"),
        P(),
        P("segment", "dp", None),
        P("segment", None, "dp"),
        P("segment", None, "dp"),
        P("segment", None, "dp"),
        P("dp", None, None),
    )
    out_specs = (P("segment", None, "dp"), P("segment", None, "dp"))
    return jax.shard_map(body, mesh=mesh, in_specs=in_specs, out_specs=out_specs, check_vma=False)
```

```python
import jax
import jax.numpy as jnp
from jax import lax
from jax.sharding import PartitionSpec as P

VIT_HEADS = 16


def as_sent(value):

    def short(part):
        return part.astype(jnp.bfloat16) if part.dtype == jnp.float32 else part

    return jax.tree.map(short, value)


def passed_along(value, axis, by):
    size = lax.axis_size(axis)
    pairs = [(i, i + by) for i in range(size) if 0 <= i + by < size]
    return lax.ppermute(value, axis, pairs)


def rms_scale(values):
    return lax.rsqrt(jnp.mean(values * values, axis=-1, keepdims=True) + 1e-06)


def segment_parts(inputs, value_full, out_full, down_full):
    widened = inputs.astype(jnp.float32)
    first_rms = rms_scale(widened)
    normed_one = (widened * first_rms).astype(jnp.bfloat16)
    valued = lax.optimization_barrier(
        jnp.dot(normed_one, value_full, preferred_element_type=jnp.float32).astype(jnp.bfloat16)
    )
    base = (widened + jnp.dot(valued, out_full, preferred_element_type=jnp.float32)).astype(
        jnp.bfloat16
    )
    base_wide = base.astype(jnp.float32)
    second_rms = rms_scale(base_wide)
    normed_two = (base_wide * second_rms).astype(jnp.bfloat16)
    before = lax.dot_general(
        normed_two, down_full, (((1,), (1,)), ((), ())), preferred_element_type=jnp.float32
    )
    return (widened, first_rms, base_wide, second_rms, normed_two, before)


def segment_forward(inputs, value_full, out_full, down_full, up_full):
    widened, first_rms, base_wide, second_rms, normed_two, before = segment_parts(
        inputs, value_full, out_full, down_full
    )
    hidden = jax.nn.silu(before).astype(jnp.bfloat16)
    return (base_wide + jnp.dot(hidden, up_full, preferred_element_type=jnp.float32)).astype(
        jnp.bfloat16
    )


def norm_back(grad_normed, widened, inverse_rms, upstream_wide):
    inner_mean = jnp.mean(grad_normed * widened, axis=-1, keepdims=True)
    cubed = inverse_rms * inverse_rms * inverse_rms
    return (upstream_wide + inverse_rms * grad_normed - widened * cubed * inner_mean).astype(
        jnp.bfloat16
    )


def transposed_dot(left, right):
    return lax.dot_general(
        left, right, (((1,), (1,)), ((), ())), preferred_element_type=jnp.float32
    )


def segment_backward(inputs, upstream, value_full, out_full, down_full, up_full):
    widened, first_rms, base_wide, second_rms, normed_two, before = segment_parts(
        inputs, value_full, out_full, down_full
    )
    hidden = jax.nn.silu(before).astype(jnp.bfloat16)
    up_term = lax.dot_general(
        hidden, upstream, (((0,), (0,)), ((), ())), preferred_element_type=jnp.float32
    )
    through = transposed_dot(upstream, up_full)
    sigmoid_part = jax.nn.sigmoid(before)
    grad_before = (through * sigmoid_part * (1.0 + before * (1.0 - sigmoid_part))).astype(
        jnp.bfloat16
    )
    down_term = lax.dot_general(
        grad_before, normed_two, (((0,), (0,)), ((), ())), preferred_element_type=jnp.float32
    )
    grad_two = jnp.dot(grad_before, down_full, preferred_element_type=jnp.float32)
    grad_base = norm_back(grad_two, base_wide, second_rms, upstream.astype(jnp.float32))
    grad_valued = lax.optimization_barrier(
        transposed_dot(grad_base, out_full).astype(jnp.bfloat16)
    )
    grad_one = transposed_dot(grad_valued, value_full)
    grad_inputs = norm_back(grad_one, widened, first_rms, grad_base.astype(jnp.float32))
    return (grad_inputs, down_term, up_term)


def segment_forward_with_base(inputs, value_full, out_full, down_full, up_full):
    widened, first_rms, base_wide, second_rms, normed_two, before = segment_parts(
        inputs, value_full, out_full, down_full
    )
    hidden = jax.nn.silu(before).astype(jnp.bfloat16)
    result = (base_wide + jnp.dot(hidden, up_full, preferred_element_type=jnp.float32)).astype(
        jnp.bfloat16
    )
    return result, base_wide.astype(jnp.bfloat16)


def base_of(inputs, value_full, out_full):
    widened = inputs.astype(jnp.float32)
    normed_one = (widened * rms_scale(widened)).astype(jnp.bfloat16)
    valued = lax.optimization_barrier(
        jnp.dot(normed_one, value_full, preferred_element_type=jnp.float32).astype(jnp.bfloat16)
    )
    return (widened + jnp.dot(valued, out_full, preferred_element_type=jnp.float32)).astype(
        jnp.bfloat16
    )


def segment_backward_saved(inputs, base, upstream, value_full, out_full, down_full, up_full):
    widened = inputs.astype(jnp.float32)
    first_rms = rms_scale(widened)
    base_wide = base.astype(jnp.float32)
    second_rms = rms_scale(base_wide)
    normed_two = (base_wide * second_rms).astype(jnp.bfloat16)
    before = lax.dot_general(
        normed_two, down_full, (((1,), (1,)), ((), ())), preferred_element_type=jnp.float32
    )
    hidden = jax.nn.silu(before).astype(jnp.bfloat16)
    up_term = lax.dot_general(
        hidden, upstream, (((0,), (0,)), ((), ())), preferred_element_type=jnp.float32
    )
    through = transposed_dot(upstream, up_full)
    sigmoid_part = jax.nn.sigmoid(before)
    grad_before = (through * sigmoid_part * (1.0 + before * (1.0 - sigmoid_part))).astype(
        jnp.bfloat16
    )
    down_term = lax.dot_general(
        grad_before, normed_two, (((0,), (0,)), ((), ())), preferred_element_type=jnp.float32
    )
    grad_two = jnp.dot(grad_before, down_full, preferred_element_type=jnp.float32)
    grad_base = norm_back(grad_two, base_wide, second_rms, upstream.astype(jnp.float32))
    grad_valued = lax.optimization_barrier(
        transposed_dot(grad_base, out_full).astype(jnp.bfloat16)
    )
    grad_one = transposed_dot(grad_valued, value_full)
    grad_inputs = norm_back(grad_one, widened, first_rms, grad_base.astype(jnp.float32))
    return (grad_inputs, down_term, up_term)


def segment_backward_head(inputs, base, upstream, value_full, out_full, down_full, up_full):
    widened = inputs.astype(jnp.float32)
    first_rms = rms_scale(widened)
    base_wide = base.astype(jnp.float32)
    second_rms = rms_scale(base_wide)
    normed_two = (base_wide * second_rms).astype(jnp.bfloat16)
    before = lax.dot_general(
        normed_two, down_full, (((1,), (1,)), ((), ())), preferred_element_type=jnp.float32
    )
    hidden = jax.nn.silu(before).astype(jnp.bfloat16)
    through = transposed_dot(upstream, up_full)
    sigmoid_part = jax.nn.sigmoid(before)
    grad_before = (through * sigmoid_part * (1.0 + before * (1.0 - sigmoid_part))).astype(
        jnp.bfloat16
    )
    grad_two = jnp.dot(grad_before, down_full, preferred_element_type=jnp.float32)
    grad_base = norm_back(grad_two, base_wide, second_rms, upstream.astype(jnp.float32))
    grad_valued = lax.optimization_barrier(
        transposed_dot(grad_base, out_full).astype(jnp.bfloat16)
    )
    grad_one = transposed_dot(grad_valued, value_full)
    grad_inputs = norm_back(grad_one, widened, first_rms, grad_base.astype(jnp.float32))
    return (grad_inputs, hidden, grad_before, normed_two)


def vision_tokens(patch_part, id_part, vit_qkv):
    samples_here, patch_len, vision_width = patch_part.shape
    head_width = vision_width // VIT_HEADS
    widened = patch_part.astype(jnp.float32)
    normed = (widened * rms_scale(widened)).astype(jnp.bfloat16)
    projected = jnp.dot(
        normed.reshape(samples_here * patch_len, vision_width),
        vit_qkv,
        preferred_element_type=jnp.float32,
    ).astype(jnp.bfloat16)
    projected = projected.reshape(samples_here, patch_len, 3, VIT_HEADS, head_width)
    query_part = projected[:, :, 0]
    key_part = projected[:, :, 1]
    value_part = projected[:, :, 2]
    scores = jnp.einsum(
        "nqhd,nkhd->nhqk", query_part, key_part, preferred_element_type=jnp.float32
    ) * head_width ** (-0.5)
    same_window = id_part[:, None, :, None] == id_part[:, None, None, :]
    weights = jnp.where(same_window, jnp.exp(scores), 0.0)
    probabilities = (weights / jnp.sum(weights, axis=-1, keepdims=True)).astype(jnp.bfloat16)
    attended = jnp.einsum(
        "nhqk,nkhd->nqhd", probabilities, value_part, preferred_element_type=jnp.float32
    )
    vit_out = (widened + attended.reshape(samples_here, patch_len, vision_width)).astype(
        jnp.bfloat16
    )
    return vit_out.reshape(samples_here, patch_len // 4, 4 * vision_width)


def take_rows(row_block, row_index):
    return jax.vmap(lambda block_one, index_one: jnp.take(block_one, index_one, axis=0))(
        row_block, row_index
    )


def join_rows(text_rows, image_rows, offsets):
    text_len = text_rows.shape[1]
    image_len = image_rows.shape[1]
    position = jnp.arange(text_len + image_len, dtype=jnp.int32)[None, :]
    begin_at = offsets[:, None]
    in_image = (position >= begin_at) & (position < begin_at + image_len)
    text_index = jnp.clip(
        jnp.where(position < begin_at, position, position - image_len), 0, text_len - 1
    )
    image_index = jnp.clip(position - begin_at, 0, image_len - 1)
    return jnp.where(
        in_image[:, :, None], take_rows(image_rows, image_index), take_rows(text_rows, text_index)
    )


def split_rows(grad_rows, offsets, text_len):
    image_len = grad_rows.shape[1] - text_len
    begin_at = offsets[:, None]
    text_position = jnp.arange(text_len, dtype=jnp.int32)[None, :]
    text_index = jnp.where(text_position < begin_at, text_position, text_position + image_len)
    image_index = begin_at + jnp.arange(image_len, dtype=jnp.int32)[None, :]
    return (take_rows(grad_rows, text_index), take_rows(grad_rows, image_index))


def reduce_over_dp(down_total, up_total):
    parts = lax.axis_size("dp")
    both = jnp.concatenate([down_total, up_total], axis=0).astype(jnp.bfloat16)
    rows, width = both.shape
    blocks = both.reshape(rows, parts, width // parts).transpose(1, 0, 2)
    received = lax.all_to_all(blocks, "dp", 0, 0, tiled=True)
    summed = received.astype(jnp.float32).sum(axis=0)
    return summed[: down_total.shape[0]], summed[down_total.shape[0] :]


def pick_one(array, index):
    return lax.dynamic_index_in_dim(array, index, 0, keepdims=False)


def body(
    text_embed,
    patches,
    window_ids,
    offsets,
    vit_qkv,
    frozen_value,
    frozen_out,
    adapter_down,
    adapter_up,
    cotangent,
):
    segment_index = lax.axis_index("segment")
    segment_count = lax.axis_size("segment")
    samples_here, text_len, model_width = text_embed.shape
    image_len = patches.shape[1] // 4
    total_len = text_len + image_len
    value_width = frozen_value.shape[2]
    rank = adapter_down.shape[1]
    packed = jnp.concatenate(
        [frozen_value[0].T, frozen_out[0], adapter_down[0], adapter_up[0]], axis=0
    )
    gathered = lax.all_gather(packed, "dp", axis=1, tiled=True)
    value_full = gathered[:value_width].T
    out_full = gathered[value_width : 2 * value_width]
    down_full = gathered[2 * value_width : 2 * value_width + rank]
    up_full = gathered[2 * value_width + rank :]
    rank_width = down_full.shape[0]
    segment_kind = jnp.where(
        segment_index == 0,
        0,
        jnp.where(segment_index == 1, 1, jnp.where(segment_index == segment_count - 1, 3, 2)),
    )

    weights = (value_full, out_full, down_full, up_full)
    branch_rows = samples_here * text_len

    def pad_rows(rows):
        filler = jnp.zeros((total_len - rows.shape[0], model_width), rows.dtype)
        return jnp.concatenate([rows, filler], axis=0)

    def split_samples(rows):
        return rows.reshape(samples_here, rows.shape[0] // samples_here, model_width)

    def vision_only(unused_arg):
        return vision_tokens(patches, window_ids, vit_qkv)

    def no_vision(unused_arg):
        return jnp.zeros((samples_here, image_len, model_width), jnp.bfloat16)

    image_tokens = lax.cond(segment_index == 0, vision_only, no_vision, 0)

    def prepare_vision(unused_arg):
        tokens = image_tokens.reshape(samples_here * image_len, model_width)
        act, base = segment_forward_with_base(tokens, *weights)
        return (image_tokens, split_samples(act), split_samples(base))

    def prepare_text(unused_arg):
        rows = text_embed.reshape(branch_rows, model_width)
        act, base = segment_forward_with_base(rows, *weights)
        return (text_embed, split_samples(act), split_samples(base))

    def prepare_none(unused_arg):
        empty = jnp.zeros((samples_here, text_len, model_width), jnp.bfloat16)
        return (empty, empty, empty)

    branch_in, branch_act, branch_base = lax.switch(
        jnp.minimum(segment_kind, 2), [prepare_vision, prepare_text, prepare_none], 0
    )

    def forward_tick(tick, received, saved_in, saved_base):
        micro = tick - segment_index
        valid = (micro >= 0) & (micro < samples_here)
        slot = jnp.clip(micro, 0, samples_here - 1)

        def forward_vision_case(unused_arg):
            return (pad_rows(pick_one(branch_act, slot)), received)

        def forward_text_case(unused_arg):
            joined = join_rows(
                pick_one(branch_act, slot)[None],
                received[:image_len][None],
                pick_one(offsets, slot)[None],
            )
            return (joined.reshape(total_len, model_width), received)

        def forward_section_case(unused_arg):
            return segment_forward_with_base(received, *weights)

        def forward_last_case(unused_arg):
            return (received, received)

        def forward_idle_case(unused_arg):
            return (received, received)

        outgoing, keep_base = lax.switch(
            jnp.where(valid, segment_kind, 4),
            [
                forward_vision_case,
                forward_text_case,
                forward_section_case,
                forward_last_case,
                forward_idle_case,
            ],
            0,
        )
        saved_in = lax.dynamic_update_index_in_dim(
            saved_in, jnp.where(valid, received, pick_one(saved_in, slot)), slot, 0
        )
        arriving = passed_along(outgoing, "segment", 1)
        keep_base = lax.cond(
            valid & (segment_kind == 3),
            lambda unused_arg: base_of(received, value_full, out_full),
            lambda unused_arg: keep_base,
            0,
        )
        saved_base = lax.dynamic_update_index_in_dim(
            saved_base, jnp.where(valid, keep_base, pick_one(saved_base, slot)), slot, 0
        )
        return (arriving, saved_in, saved_base)

    def backward_tick(phase, received, saved_in, saved_base, totals):
        micro = phase - (segment_count - 1 - segment_index)
        valid = (micro >= 0) & (micro < samples_here)
        slot = jnp.clip(micro, 0, samples_here - 1)

        def pad_any(rows):
            filler = jnp.zeros((total_len - rows.shape[0], rows.shape[1]), rows.dtype)
            return jnp.concatenate([rows, filler], axis=0)

        def head_padded(inputs, base, upstream):
            grad_inputs, hidden, grad_before, normed_two = segment_backward_head(
                inputs, base, upstream, *weights
            )
            return (pad_any(hidden), pad_any(grad_before), pad_rows(normed_two), pad_rows(upstream))

        small_zeros = jnp.zeros((total_len, rank_width), jnp.bfloat16)
        wide_zeros = jnp.zeros((total_len, model_width), jnp.bfloat16)

        def backward_vision_case(unused_arg):
            return (wide_zeros, small_zeros, small_zeros, wide_zeros, received)

        def backward_text_case(unused_arg):
            text_part, image_part = split_rows(
                received[None], pick_one(offsets, slot)[None], text_len
            )
            return (pad_rows(image_part[0]), small_zeros, small_zeros, wide_zeros, pad_rows(text_part[0]))

        def section_common(upstream):
            grad_inputs, hidden, grad_before, normed_two = segment_backward_head(
                pick_one(saved_in, slot), pick_one(saved_base, slot), upstream, *weights
            )
            return (grad_inputs, hidden, grad_before, normed_two, upstream)

        def backward_section_case(unused_arg):
            return section_common(received)

        def backward_last_case(unused_arg):
            return section_common(pick_one(cotangent, slot))

        def backward_idle_case(unused_arg):
            return (received, small_zeros, small_zeros, jnp.zeros_like(received), jnp.zeros_like(received))

        outgoing, hidden, grad_before, normed_two, upstream = lax.switch(
            jnp.where(valid, segment_kind, 4),
            [
                backward_vision_case,
                backward_text_case,
                backward_section_case,
                backward_last_case,
                backward_idle_case,
            ],
            0,
        )
        arriving = passed_along(outgoing, "segment", -1)

        def branch_head(unused_arg):
            return head_padded(pick_one(branch_in, slot), pick_one(branch_base, slot), upstream[:text_len])

        def branch_pass(unused_arg):
            return (hidden, grad_before, normed_two, upstream)

        hidden, grad_before, normed_two, upstream = lax.switch(
            jnp.where(valid & (segment_kind < 2), 0, 1), [branch_head, branch_pass], 0
        )
        up_term = lax.dot_general(
            hidden, upstream, (((0,), (0,)), ((), ())), preferred_element_type=jnp.float32
        )
        down_term = lax.dot_general(
            grad_before, normed_two, (((0,), (0,)), ((), ())), preferred_element_type=jnp.float32
        )
        totals = (totals[0] + down_term, totals[1] + up_term)
        return (arriving, totals)

    empty_rows = jnp.zeros((total_len, model_width), jnp.bfloat16)
    saved_start = jnp.zeros((samples_here, total_len, model_width), jnp.bfloat16)
    totals_start = (
        jnp.zeros((rank_width, model_width), jnp.float32),
        jnp.zeros((rank_width, model_width), jnp.float32),
    )
    sweep_ticks = samples_here + segment_count - 1

    def forward_step(tick, carry):
        return forward_tick(tick, carry[0], carry[1], carry[2])

    unused_rows, saved_in, saved_base = lax.fori_loop(
        0, sweep_ticks, forward_step, (empty_rows, saved_start, saved_start)
    )

    def backward_step(tick, carry):
        return backward_tick(tick, carry[0], saved_in, saved_base, carry[1])

    unused_grad, totals = lax.fori_loop(0, sweep_ticks, backward_step, (empty_rows, totals_start))
    reduced_down, reduced_up = reduce_over_dp(totals[0], totals[1])
    return (reduced_down[None], reduced_up[None])


def solution(mesh):
    in_specs = (
        P("dp", None, None),
        P("dp", None, None),
        P("dp", None),
        P("dp"),
        P(),
        P("segment", "dp", None),
        P("segment", None, "dp"),
        P("segment", None, "dp"),
        P("segment", None, "dp"),
        P("dp", None, None),
    )
    out_specs = (P("segment", None, "dp"), P("segment", None, "dp"))
    return jax.shard_map(body, mesh=mesh, in_specs=in_specs, out_specs=out_specs, check_vma=False)
```
